256 devices in a mesh: scen: 8 (over y, z_hi), grid: 32 (over x, z_lo, core).
Axes of the slice: x: 4, y: 4, z: 8 (z_hi: 2, z_lo: 4; z = z_hi * 4 + z_lo), core: 2. Of those that a mesh axis runs over, the one named last changes fastest.
Arguments:
- adjoint_in: float32 [16, 2, 50, 512, 128], P('scen', None, None, 'grid'), may hold values from -6 to 6
- surface_carbon: float32 [16, 512, 128], P('scen', 'grid'), may hold values from 1.9 to 2.1
- surface_alkalinity: float32 [16, 512, 128], P('scen', 'grid'), may hold values from 2.2 to 2.4
- east_velocity: float32 [50, 512, 128], P(None, 'grid'), may hold values from -0.1 to 0.1
- north_velocity: float32 [50, 512, 128], P(None, 'grid'), may hold values from -0.1 to 0.1
- east_diffusion: float32 [50], replicated, may hold values from 0.08 to 0.25
- north_diffusion: float32 [50], replicated, may hold values from 0.02 to 0.1
- vertical_mix: float32 [50, 512, 128], P(None, 'grid'), may hold values from 0.05 to 5
- thickness: float32 [50], replicated, may hold values from 0.5 to 4
- export_flux: float32 [50, 512, 128], P(None, 'grid'), may hold values from 0.1 to 1
- piston: float32 [512, 128], P('grid'), may hold values from 0.0005 to 0.005
- wet_mask: int32 [512, 128], P('grid'), may hold values 0 or 1
- bottom_level: int32 [512, 128], P('grid'), may hold values from 41 to 50
Outputs:
- adjoint_out: float32 [16, 2, 50, 512, 128], P('scen', None, None, 'grid')
- rate_gradient: float32 [50, 512, 128], P(None, 'grid')
The draws below stay inside these ranges and needn't reach their ends.
All inputs are finite; a program needn't handle non-finite values. No bound on the sum of `wet_mask` on one device may be relied on, other than what follows from the above.
Results may differ from the reference program's by a relative error of at most 0.00002.
Values sent between devices are 32-bit elements; how exact they have to be, the bound alone decides.
No kernel may reach another device: no remote copies, remote signals or barrier semaphores. Data moves between devices by JAX's collectives and lax.ppermute only.
A program may use at most 64 MiB of HBM per device.

```python
import math
import jax
import jax.numpy as jnp
from jax import lax

LEVELS = 50
LATS = 128
SUBSTEPS = 6
LONS = 512
SCENARIOS = 16


def plant(array, own_key, smallest, largest):
    longest = array.shape.index(max(array.shape))
    spots = []
    for shift in (0, 1):
        where = [jax.random.randint(jax.random.fold_in(own_key, axis), (), 0, length) for axis, length in enumerate(array.shape)]
        where[longest] = (where[longest] + shift) % array.shape[longest]
        spots.append(tuple(where))
    return array.at[spots[0]].set(smallest).at[spots[1]].set(largest)


def block_scale(own_key, dims, shards, smallest, high):
    gain, own = 1.0, jax.random.fold_in(own_key, 6)
    for axis_at, blocks in shards:
        steps = jnp.exp(jax.random.uniform(jax.random.fold_in(own, axis_at), (blocks,), jnp.float32, smallest / len(shards), high / len(shards)))
        gain = gain * jnp.repeat(steps, dims[axis_at] // blocks).reshape([-1 if axis == axis_at else 1 for axis in range(len(dims))])
    return gain


def noise(rng, dims, scale, most, shards=(), held_as=jnp.bfloat16):
    drawn = scale * jax.random.normal(rng, dims, jnp.float32)
    if shards:
        drawn = drawn * block_scale(rng, dims, shards, -0.22, 0.18)
    return jnp.clip(drawn, -most, most).astype(held_as)


def setup_inputs(seed: int = 0) -> dict:
    key_list = jax.random.split(jax.random.key(seed), 14)
    return {
        "adjoint_in": noise(key_list[0], (SCENARIOS, 2, LEVELS, LONS, LATS), 1.0, 6.0, ((0, 8), (3, 32)), jnp.float32),
        "surface_carbon": jnp.clip(1.9 + 0.19999993 * jax.random.uniform(key_list[1], (SCENARIOS, LONS, LATS), jnp.float32) ** block_scale(key_list[1], (SCENARIOS, LONS, LATS), ((0, 8), (1, 32)), -0.2, 0.2), 1.9, 2.1),
        "surface_alkalinity": jnp.clip(2.2 + 0.20000005 * jax.random.uniform(key_list[2], (SCENARIOS, LONS, LATS), jnp.float32) ** block_scale(key_list[2], (SCENARIOS, LONS, LATS), ((0, 8), (1, 32)), -0.2, 0.2), 2.2, 2.4),
        "east_velocity": jnp.clip(jax.random.uniform(key_list[3], (LEVELS, LONS, LATS), jnp.float32, -0.1, 0.1) * block_scale(key_list[3], (LEVELS, LONS, LATS), ((1, 32),), -0.4, 0.0), -0.1, 0.1),
        "north_velocity": jnp.clip(jax.random.uniform(key_list[4], (LEVELS, LONS, LATS), jnp.float32, -0.1, 0.1) * block_scale(key_list[4], (LEVELS, LONS, LATS), ((1, 32),), -0.4, 0.0), -0.1, 0.1),
        "east_diffusion": jnp.clip(jnp.exp(jax.random.uniform(key_list[5], (LEVELS,), jnp.float32, math.log(0.08), math.log(0.25))), 0.08, 0.25),
        "north_diffusion": jnp.clip(jnp.exp(jax.random.uniform(key_list[6], (LEVELS,), jnp.float32, math.log(0.02), math.log(0.1))), 0.02, 0.1),
        "vertical_mix": jnp.clip(jnp.exp(math.log(5.0) - 4.6051702 * jax.random.uniform(key_list[7], (LEVELS, LONS, LATS), jnp.float32) ** block_scale(key_list[7], (LEVELS, LONS, LATS), ((1, 32),), -0.2, 0.2)), 0.05, 5.0),
        "thickness": jnp.clip(jnp.exp(jax.random.uniform(key_list[8], (LEVELS,), jnp.float32, math.log(0.5), math.log(4.0))), 0.5, 4.0),
        "export_flux": jnp.clip(jnp.exp(math.log(1.0) - 2.3025851 * jax.random.uniform(key_list[9], (LEVELS, LONS, LATS), jnp.float32) ** block_scale(key_list[9], (LEVELS, LONS, LATS), ((1, 32),), -0.2, 0.2)), 0.1, 1.0),
        "piston": jnp.clip(jnp.exp(math.log(0.005) - 2.30258502 * jax.random.uniform(key_list[10], (LONS, LATS), jnp.float32) ** block_scale(key_list[10], (LONS, LATS), ((0, 32),), -0.2, 0.2)), 0.0005, 0.005),
        "wet_mask": plant((jax.random.randint(key_list[11], (LONS, LATS), 0, 10) < 9).astype(jnp.int32), jax.random.fold_in(key_list[11], 1), 0, 1),
        "bottom_level": plant(jax.random.randint(key_list[12], (LONS, LATS), LEVELS - 9, LEVELS + 1), jax.random.fold_in(key_list[12], 1), LEVELS - 9, LEVELS).astype(jnp.int32),
    }


alk_ratio = 0.137

def wet_cells(wet_mask, bottom_level, levels):
    depth_index = lax.broadcasted_iota(jnp.int32, (levels,) + wet_mask.shape, 0)
    return ((wet_mask[None] > 0) & (depth_index < bottom_level[None])).astype(jnp.float32)

def face_pairs(velocity, mask_here, mask_next, diffusion):
    opened = mask_here * mask_next
    moving = velocity * opened
    mixing = diffusion[:, None, None] * opened
    return (mixing + jnp.maximum(moving, 0.0), jnp.minimum(moving, 0.0) - mixing)

def north_flux(tracer, upwind, downwind):
    north_faces = upwind * tracer[..., :-1] + downwind * tracer[..., 1:]
    zero_column = jnp.zeros(north_faces.shape[:-1] + (1,), jnp.float32)
    return jnp.concatenate([north_faces, zero_column], -1) - jnp.concatenate([zero_column, north_faces], -1)

def column_coefficients(vertical_mix, thickness, wet_cube):
    zero_layer = jnp.zeros((1,) + wet_cube.shape[1:], jnp.float32)
    opened = jnp.concatenate([wet_cube[:-1] * wet_cube[1:], zero_layer], 0)
    mixing = vertical_mix * opened
    mixing_above = jnp.concatenate([zero_layer, mixing[:-1]], 0)
    height = thickness[:, None, None]
    height_above = jnp.concatenate([thickness[:1], thickness[:-1]])[:, None, None]
    height_below = jnp.concatenate([thickness[1:], thickness[-1:]])[:, None, None]
    diagonal = 1.0 + (mixing + mixing_above) / height
    below_band = -mixing_above / height_above
    above_band = -mixing / height_below
    return (below_band, diagonal, above_band)

def transposed_solve(right_side, below_band, diagonal, above_band):
    levels = diagonal.shape[0]
    pivots = diagonal[0]
    factors = [above_band[0] / pivots]
    reduced = [right_side[..., 0, :, :] / pivots]
    for level in range(1, levels):
        pivots = diagonal[level] - below_band[level] * factors[-1]
        factors.append(above_band[level] / pivots)
        reduced.append((right_side[..., level, :, :] - below_band[level] * reduced[-1]) / pivots)
    solved = [reduced[-1]]
    for level in range(levels - 2, -1, -1):
        solved.append(reduced[level] - factors[level] * solved[-1])
    return jnp.stack(solved[::-1], axis=-3)

def carbonate_slopes(carbon, alkalinity):
    excess = 2.0 * carbon - alkalinity
    spread = alkalinity - carbon
    square = spread * spread
    return ((4.0 * excess * spread + excess * excess) / square, (-2.0 * excess * spread - excess * excess) / square)

def reference(adjoint_in, surface_carbon, surface_alkalinity, east_velocity, north_velocity, east_diffusion, north_diffusion, vertical_mix, thickness, export_flux, piston, wet_mask, bottom_level):
    levels = vertical_mix.shape[0]
    wet_cube = wet_cells(wet_mask, bottom_level, levels)
    below_band, diagonal, above_band = column_coefficients(vertical_mix, thickness, wet_cube)
    east_a, east_b = face_pairs(east_velocity, wet_cube, jnp.roll(wet_cube, -1, 1), east_diffusion)
    north_a, north_b = face_pairs(north_velocity[:, :, :-1], wet_cube[:, :, :-1], wet_cube[:, :, 1:], north_diffusion)

    def substep(tracer):
        east_flux = east_a * tracer + east_b * jnp.roll(tracer, -1, -2)
        return tracer - (east_flux - jnp.roll(east_flux, 1, -2)) - north_flux(tracer, north_a, north_b)

    def one_scenario(inputs):
        cotangent, carbon, alkalinity = inputs
        adjoint = transposed_solve(cotangent, below_band, diagonal, above_band)
        pullback = jax.vjp(substep, jnp.zeros_like(adjoint))[1]
        for repeat in range(SUBSTEPS):
            adjoint = pullback(adjoint)[0]
        rate_term = adjoint[0] - alk_ratio * adjoint[1]
        slope_carbon, slope_alkalinity = carbonate_slopes(carbon, alkalinity)
        exchange_scale = wet_cube[0] * piston * adjoint[0, 0]
        adjoint = adjoint.at[0, 0].add(-exchange_scale * slope_carbon).at[1, 0].add(-exchange_scale * slope_alkalinity)
        return (adjoint, rate_term)
    adjoints, rate_terms = lax.map(one_scenario, (adjoint_in, surface_carbon, surface_alkalinity))
    rate_gradient = export_flux * wet_cube * lax.optimization_barrier(jnp.sum(rate_terms, axis=0))
    return (adjoints, rate_gradient)
```

```python
import jax
import jax.numpy as jnp
from jax import lax
from jax.sharding import PartitionSpec as P

SUBSTEPS = 6


alk_ratio = 0.137


def widened(array, dim, width):
    size, length = (lax.axis_size("grid"), array.shape[dim])
    up = [(i, (i + 1) % size) for i in range(size)]
    down = [(j, i) for i, j in up]
    last = lax.slice_in_dim(array, length - width, length, axis=dim)
    initial = lax.slice_in_dim(array, 0, width, axis=dim)
    before = lax.ppermute(last, "grid", up)
    after = lax.ppermute(initial, "grid", down)
    return jnp.concatenate([before, array, after], axis=dim)


def face_pairs(velocity, mask_here, mask_next, diffusion):
    opened = mask_here * mask_next
    moving = velocity * opened
    mixing = diffusion[:, None, None] * opened
    return (mixing + jnp.maximum(moving, 0.0), jnp.minimum(moving, 0.0) - mixing)


def north_transpose(adjoint, upwind, downwind):
    zero_column = jnp.zeros(adjoint.shape[:-1] + (1,), jnp.float32)
    zero_face = jnp.zeros(upwind.shape[:-1] + (1,), jnp.float32)
    ahead = jnp.concatenate([adjoint[..., 1:], zero_column], -1)
    behind = jnp.concatenate([zero_column, adjoint[..., :-1]], -1)
    upwind_full = jnp.concatenate([upwind, zero_face], -1)
    downwind_full = jnp.concatenate([zero_face, downwind], -1)
    return upwind_full * (adjoint - ahead) + downwind_full * (behind - adjoint)


def column_coefficients(vertical_mix, thickness, wet_cube):
    zero_layer = jnp.zeros((1,) + wet_cube.shape[1:], jnp.float32)
    opened = jnp.concatenate([wet_cube[:-1] * wet_cube[1:], zero_layer], 0)
    mixing = vertical_mix * opened
    mixing_above = jnp.concatenate([zero_layer, mixing[:-1]], 0)
    height = thickness[:, None, None]
    height_above = jnp.concatenate([thickness[:1], thickness[:-1]])[:, None, None]
    height_below = jnp.concatenate([thickness[1:], thickness[-1:]])[:, None, None]
    diagonal = 1.0 + (mixing + mixing_above) / height
    below_band = -mixing_above / height_above
    above_band = -mixing / height_below
    return (below_band, diagonal, above_band)


def transposed_solve(right_side, below_band, diagonal, above_band):
    levels = diagonal.shape[0]
    pivots = diagonal[0]
    factors = [above_band[0] / pivots]
    reduced = [right_side[..., 0, :, :] / pivots]
    for level in range(1, levels):
        pivots = diagonal[level] - below_band[level] * factors[-1]
        factors.append(above_band[level] / pivots)
        reduced.append((right_side[..., level, :, :] - below_band[level] * reduced[-1]) / pivots)
    solved = [reduced[-1]]
    for level in range(levels - 2, -1, -1):
        solved.append(reduced[level] - factors[level] * solved[-1])
    return jnp.stack(solved[::-1], axis=-3)


def carbonate_slopes(carbon, alkalinity):
    excess = 2.0 * carbon - alkalinity
    spread = alkalinity - carbon
    square = spread * spread
    return (
        (4.0 * excess * spread + excess * excess) / square,
        (-2.0 * excess * spread - excess * excess) / square,
    )


def scenario_sum(field):
    size = lax.axis_size("scen")
    index = lax.axis_index("scen")
    shape = field.shape
    rows = field.reshape(-1, shape[-1])
    bits = [b for b in (2, 4, 1) if b < size]
    bits += [b for b in (8, 16, 32) if b < size]
    kept_bits = []
    for bit in bits:
        half = rows.shape[0] // 2
        upper = (index // bit) % 2 == 1
        low, high = rows[:half], rows[half:]
        keep = jnp.where(upper, high, low)
        send = jnp.where(upper, low, high)
        pairs = [(i, i ^ bit) for i in range(size)]
        rows = keep + lax.ppermute(send, "scen", pairs)
        kept_bits.append((bit, upper))
    for bit, upper in kept_bits[::-1]:
        pairs = [(i, i ^ bit) for i in range(size)]
        other = lax.ppermute(rows, "scen", pairs)
        rows = jnp.where(
            upper,
            jnp.concatenate([other, rows], 0),
            jnp.concatenate([rows, other], 0),
        )
    return rows.reshape(shape)


def on_device(
    adjoint_in,
    surface_carbon,
    surface_alkalinity,
    east_velocity,
    north_velocity,
    east_diffusion,
    north_diffusion,
    vertical_mix,
    thickness,
    export_flux,
    piston,
    wet_mask,
    bottom_level,
):
    levels = vertical_mix.shape[0]
    width = east_velocity.shape[1]
    halo = SUBSTEPS
    wet_bottom = jnp.where(wet_mask > 0, bottom_level, 0)
    wide_bottom = widened(wet_bottom, 0, halo)
    wide_east = widened(east_velocity, 1, halo)
    wide_north = widened(north_velocity, 1, halo)
    depth_index = lax.broadcasted_iota(jnp.int32, (levels,) + wide_bottom.shape, 0)
    wide_wet = (depth_index < wide_bottom[None]).astype(jnp.float32)
    wet_cube = wide_wet[:, halo : halo + width]

    below_band, diagonal, above_band = column_coefficients(vertical_mix, thickness, wet_cube)
    adjoint = transposed_solve(adjoint_in, below_band, diagonal, above_band)
    adjoint = widened(adjoint, 3, halo)

    east_a, east_b = face_pairs(
        wide_east[:, :-1], wide_wet[:, :-1], wide_wet[:, 1:], east_diffusion
    )
    north_a, north_b = face_pairs(
        wide_north[:, :, :-1], wide_wet[:, :, :-1], wide_wet[:, :, 1:], north_diffusion
    )
    total = width + 2 * halo
    for repeat in range(SUBSTEPS):
        first, stop = repeat + 1, total - repeat - 1
        centre = adjoint[..., 1:-1, :]
        adjoint = (
            centre
            - east_a[:, first:stop] * (centre - adjoint[..., 2:, :])
            - east_b[:, first - 1 : stop - 1] * (adjoint[..., :-2, :] - centre)
            - north_transpose(centre, north_a[:, first:stop], north_b[:, first:stop])
        )
    rate_term = jnp.sum(adjoint[:, 0] - alk_ratio * adjoint[:, 1], axis=0)
    summed = scenario_sum(rate_term)
    rate_gradient = export_flux * wet_cube * summed
    slope_carbon, slope_alkalinity = carbonate_slopes(surface_carbon, surface_alkalinity)
    exchange_scale = wet_cube[0] * piston * adjoint[:, 0, 0]
    adjoint = (
        adjoint.at[:, 0, 0]
        .add(-exchange_scale * slope_carbon)
        .at[:, 1, 0]
        .add(-exchange_scale * slope_alkalinity)
    )
    return (adjoint, rate_gradient)


def solution(mesh):
    in_specs = (
        P("scen", None, None, "grid", None),
        P("scen", "grid", None),
        P("scen", "grid", None),
        P(None, "grid", None),
        P(None, "grid", None),
        P(),
        P(),
        P(None, "grid", None),
        P(),
        P(None, "grid", None),
        P("grid", None),
        P("grid", None),
        P("grid", None),
    )
    out_specs = (P("scen", None, None, "grid", None), P(None, "grid", None))
    return jax.shard_map(
        on_device, mesh=mesh, in_specs=in_specs, out_specs=out_specs, check_vma=False
    )
```

```python
import jax
import jax.numpy as jnp
from jax import lax
from jax.sharding import PartitionSpec as P

SUBSTEPS = 6


alk_ratio = 0.137


def widened(array, dim, width):
    size, length = (lax.axis_size("grid"), array.shape[dim])
    up = [(i, (i + 1) % size) for i in range(size)]
    down = [(j, i) for i, j in up]
    last = lax.slice_in_dim(array, length - width, length, axis=dim)
    initial = lax.slice_in_dim(array, 0, width, axis=dim)
    before = lax.ppermute(last, "grid", up)
    after = lax.ppermute(initial, "grid", down)
    return jnp.concatenate([before, array, after], axis=dim)


def face_pairs(velocity, mask_here, mask_next, diffusion):
    opened = mask_here * mask_next
    moving = velocity * opened
    mixing = diffusion[:, None, None] * opened
    return (mixing + jnp.maximum(moving, 0.0), jnp.minimum(moving, 0.0) - mixing)


def north_transpose(adjoint, upwind, downwind):
    zero_column = jnp.zeros(adjoint.shape[:-1] + (1,), jnp.float32)
    zero_face = jnp.zeros(upwind.shape[:-1] + (1,), jnp.float32)
    ahead = jnp.concatenate([adjoint[..., 1:], zero_column], -1)
    behind = jnp.concatenate([zero_column, adjoint[..., :-1]], -1)
    upwind_full = jnp.concatenate([upwind, zero_face], -1)
    downwind_full = jnp.concatenate([zero_face, downwind], -1)
    return upwind_full * (adjoint - ahead) + downwind_full * (behind - adjoint)


def column_coefficients(vertical_mix, thickness, wet_cube):
    zero_layer = jnp.zeros((1,) + wet_cube.shape[1:], jnp.float32)
    opened = jnp.concatenate([wet_cube[:-1] * wet_cube[1:], zero_layer], 0)
    mixing = vertical_mix * opened
    mixing_above = jnp.concatenate([zero_layer, mixing[:-1]], 0)
    height = thickness[:, None, None]
    height_above = jnp.concatenate([thickness[:1], thickness[:-1]])[:, None, None]
    height_below = jnp.concatenate([thickness[1:], thickness[-1:]])[:, None, None]
    diagonal = 1.0 + (mixing + mixing_above) / height
    below_band = -mixing_above / height_above
    above_band = -mixing / height_below
    return (below_band, diagonal, above_band)


def elimination(below_band, diagonal, above_band):
    levels = diagonal.shape[0]
    pivots = [diagonal[0]]
    factors = [above_band[0] / pivots[0]]
    for level in range(1, levels):
        pivots.append(diagonal[level] - below_band[level] * factors[-1])
        factors.append(above_band[level] / pivots[-1])
    return pivots, factors


def transposed_solve(right_side, below_band, pivots, factors):
    levels = len(pivots)
    reduced = [right_side[..., 0, :, :] / pivots[0]]
    for level in range(1, levels):
        reduced.append((right_side[..., level, :, :] - below_band[level] * reduced[-1]) / pivots[level])
    solved = [reduced[-1]]
    for level in range(levels - 2, -1, -1):
        solved.append(reduced[level] - factors[level] * solved[-1])
    return jnp.stack(solved[::-1], axis=-3)


def carbonate_slopes(carbon, alkalinity):
    excess = 2.0 * carbon - alkalinity
    spread = alkalinity - carbon
    square = spread * spread
    return (
        (4.0 * excess * spread + excess * excess) / square,
        (-2.0 * excess * spread - excess * excess) / square,
    )


def scenario_sum(field):
    size = lax.axis_size("scen")
    index = lax.axis_index("scen")
    shape = field.shape
    rows = field.reshape(-1, shape[-1])
    bits = [b for b in (2, 4, 1) if b < size]
    bits += [b for b in (8, 16, 32) if b < size]
    kept_bits = []
    for bit in bits:
        half = rows.shape[0] // 2
        upper = (index // bit) % 2 == 1
        low, high = rows[:half], rows[half:]
        keep = jnp.where(upper, high, low)
        send = jnp.where(upper, low, high)
        pairs = [(i, i ^ bit) for i in range(size)]
        rows = keep + lax.ppermute(send, "scen", pairs)
        kept_bits.append((bit, upper))
    for bit, upper in kept_bits[::-1]:
        pairs = [(i, i ^ bit) for i in range(size)]
        other = lax.ppermute(rows, "scen", pairs)
        rows = jnp.where(
            upper,
            jnp.concatenate([other, rows], 0),
            jnp.concatenate([rows, other], 0),
        )
    return rows.reshape(shape)


def transport_transpose(adjoint, east_a, east_b_behind, north_a, north_b_behind):
    ahead = jnp.roll(adjoint, -1, axis=-2)
    behind = jnp.roll(adjoint, 1, axis=-2)
    north_ahead = jnp.roll(adjoint, -1, axis=-1)
    north_behind = jnp.roll(adjoint, 1, axis=-1)
    return (
        adjoint
        - east_a * (adjoint - ahead)
        - east_b_behind * (behind - adjoint)
        - (north_a * (adjoint - north_ahead) + north_b_behind * (north_behind - adjoint))
    )


def on_device(
    adjoint_in,
    surface_carbon,
    surface_alkalinity,
    east_velocity,
    north_velocity,
    east_diffusion,
    north_diffusion,
    vertical_mix,
    thickness,
    export_flux,
    piston,
    wet_mask,
    bottom_level,
):
    levels = vertical_mix.shape[0]
    width = east_velocity.shape[1]
    halo = SUBSTEPS
    padded = -(-(width + 2 * halo) // 8) * 8
    wet_bottom = jnp.where(wet_mask > 0, bottom_level, 0).astype(jnp.float32)
    pieces = [
        adjoint_in.reshape((-1,) + adjoint_in.shape[-2:]),
        east_velocity,
        north_velocity,
        vertical_mix,
        wet_bottom[None],
    ]
    sizes = [piece.shape[0] for piece in pieces]
    size = lax.axis_size("grid")
    up = [(i, (i + 1) % size) for i in range(size)]
    down = [(j, i) for i, j in up]
    last = jnp.concatenate([piece[:, width - halo :] for piece in pieces], 0)
    initial = jnp.concatenate([piece[:, :halo] for piece in pieces], 0)
    before = lax.ppermute(last, "grid", up)
    after = lax.ppermute(initial, "grid", down)
    wide = []
    offset = 0
    for piece, rows in zip(pieces, sizes):
        fill = jnp.zeros((rows, padded - width - 2 * halo, piece.shape[-1]), jnp.float32)
        wide.append(
            jnp.concatenate(
                [before[offset : offset + rows], piece, after[offset : offset + rows], fill], 1
            )
        )
        offset += rows
    wide_in, wide_east, wide_north, wide_mix, wide_bottom = wide
    wide_in = wide_in.reshape(adjoint_in.shape[:-2] + wide_in.shape[-2:])
    depth_index = lax.broadcasted_iota(jnp.int32, (levels,) + wide_bottom.shape[1:], 0)
    wide_wet = (depth_index.astype(jnp.float32) < wide_bottom).astype(jnp.float32)
    wet_cube = wide_wet[:, halo : halo + width]

    below_band, diagonal, above_band = column_coefficients(wide_mix, thickness, wide_wet)
    pivots, factors = elimination(below_band, diagonal, above_band)

    east_a, east_b = face_pairs(
        wide_east, wide_wet, jnp.roll(wide_wet, -1, axis=1), east_diffusion
    )
    zero_row = jnp.zeros(wide_wet.shape[:-1] + (1,), jnp.float32)
    north_next = jnp.concatenate([wide_wet[..., 1:], zero_row], -1)
    north_a, north_b = face_pairs(wide_north, wide_wet, north_next, north_diffusion)
    coefficients = (
        east_a,
        jnp.roll(east_b, 1, axis=1),
        north_a,
        jnp.roll(north_b, 1, axis=-1),
    )

    combined = jnp.sum(wide_in[:, 0] - alk_ratio * wide_in[:, 1], axis=0)
    combined = scenario_sum(combined)
    combined = transposed_solve(combined, below_band, pivots, factors)
    adjoint = transposed_solve(wide_in, below_band, pivots, factors)
    for repeat in range(SUBSTEPS):
        adjoint = transport_transpose(adjoint, *coefficients)
        combined = transport_transpose(combined, *coefficients)
    adjoint = adjoint[..., halo : halo + width, :]
    summed = combined[:, halo : halo + width]
    rate_gradient = export_flux * wet_cube * summed
    slope_carbon, slope_alkalinity = carbonate_slopes(surface_carbon, surface_alkalinity)
    exchange_scale = wet_cube[0] * piston * adjoint[:, 0, 0]
    adjoint = (
        adjoint.at[:, 0, 0]
        .add(-exchange_scale * slope_carbon)
        .at[:, 1, 0]
        .add(-exchange_scale * slope_alkalinity)
    )
    return (adjoint, rate_gradient)


def solution(mesh):
    in_specs = (
        P("scen", None, None, "grid", None),
        P("scen", "grid", None),
        P("scen", "grid", None),
        P(None, "grid", None),
        P(None, "grid", None),
        P(),
        P(),
        P(None, "grid", None),
        P(),
        P(None, "grid", None),
        P("grid", None),
        P("grid", None),
        P("grid", None),
    )
    out_specs = (P("scen", None, None, "grid", None), P(None, "grid", None))
    return jax.shard_map(
        on_device, mesh=mesh, in_specs=in_specs, out_specs=out_specs, check_vma=False
    )
```

```python
import jax
import jax.numpy as jnp
from jax import lax
from jax.sharding import PartitionSpec as P
from jax.experimental import pallas as pl
from jax.experimental.pallas import tpu as pltpu

SUBSTEPS = 6


alk_ratio = 0.137


def face_pairs(velocity, mask_here, mask_next, diffusion):
    opened = mask_here * mask_next
    moving = velocity * opened
    mixing = diffusion[:, None, None] * opened
    return (mixing + jnp.maximum(moving, 0.0), jnp.minimum(moving, 0.0) - mixing)


def column_coefficients(vertical_mix, thickness, wet_cube):
    zero_layer = jnp.zeros((1,) + wet_cube.shape[1:], jnp.float32)
    opened = jnp.concatenate([wet_cube[:-1] * wet_cube[1:], zero_layer], 0)
    mixing = vertical_mix * opened
    mixing_above = jnp.concatenate([zero_layer, mixing[:-1]], 0)
    height = thickness[:, None, None]
    height_above = jnp.concatenate([thickness[:1], thickness[:-1]])[:, None, None]
    height_below = jnp.concatenate([thickness[1:], thickness[-1:]])[:, None, None]
    diagonal = 1.0 + (mixing + mixing_above) / height
    below_band = -mixing_above / height_above
    above_band = -mixing / height_below
    return (below_band, diagonal, above_band)


def elimination(below_band, diagonal, above_band):
    levels = diagonal.shape[0]
    pivots = [diagonal[0]]
    factors = [above_band[0] / pivots[0]]
    for level in range(1, levels):
        pivots.append(diagonal[level] - below_band[level] * factors[-1])
        factors.append(above_band[level] / pivots[-1])
    return pivots, factors


def transposed_solve(right_side, below_band, pivots, factors):
    levels = len(pivots)
    reduced = [right_side[..., 0, :, :] / pivots[0]]
    for level in range(1, levels):
        reduced.append((right_side[..., level, :, :] - below_band[level] * reduced[-1]) / pivots[level])
    solved = [reduced[-1]]
    for level in range(levels - 2, -1, -1):
        solved.append(reduced[level] - factors[level] * solved[-1])
    return jnp.stack(solved[::-1], axis=-3)


def carbonate_slopes(carbon, alkalinity):
    excess = 2.0 * carbon - alkalinity
    spread = alkalinity - carbon
    square = spread * spread
    return (
        (4.0 * excess * spread + excess * excess) / square,
        (-2.0 * excess * spread - excess * excess) / square,
    )


def scenario_sum(field):
    size = lax.axis_size("scen")
    index = lax.axis_index("scen")
    shape = field.shape
    rows = field.reshape(-1, shape[-1])
    bits = [b for b in (2, 4, 1) if b < size]
    bits += [b for b in (8, 16, 32) if b < size]
    kept_bits = []
    for bit in bits:
        half = rows.shape[0] // 2
        upper = (index // bit) % 2 == 1
        low, high = rows[:half], rows[half:]
        keep = jnp.where(upper, high, low)
        send = jnp.where(upper, low, high)
        pairs = [(i, i ^ bit) for i in range(size)]
        rows = keep + lax.ppermute(send, "scen", pairs)
        kept_bits.append((bit, upper))
    for bit, upper in kept_bits[::-1]:
        pairs = [(i, i ^ bit) for i in range(size)]
        other = lax.ppermute(rows, "scen", pairs)
        rows = jnp.where(
            upper,
            jnp.concatenate([other, rows], 0),
            jnp.concatenate([rows, other], 0),
        )
    return rows.reshape(shape)


def substep_kernel(adjoint_ref, east_a_ref, east_b_ref, north_a_ref, north_b_ref, out_ref):
    columns = adjoint_ref.shape[-2]
    lanes = adjoint_ref.shape[-1]
    east_a = east_a_ref[...]
    east_b_behind = pltpu.roll(east_b_ref[...], 1, 1)
    north_a = north_a_ref[...]
    north_b_behind = pltpu.roll(north_b_ref[...], 1, 2)
    for field in range(adjoint_ref.shape[0]):
        adjoint = adjoint_ref[field]
        for repeat in range(SUBSTEPS):
            ahead = pltpu.roll(adjoint, columns - 1, 1)
            behind = pltpu.roll(adjoint, 1, 1)
            north_ahead = pltpu.roll(adjoint, lanes - 1, 2)
            north_behind = pltpu.roll(adjoint, 1, 2)
            adjoint = (
                adjoint
                - east_a * (adjoint - ahead)
                - east_b_behind * (behind - adjoint)
                - (north_a * (adjoint - north_ahead) + north_b_behind * (north_behind - adjoint))
            )
        aligned = pltpu.roll(adjoint, columns - SUBSTEPS, 1)
        out_ref[field] = aligned[:, : out_ref.shape[-2]]


def transport_substeps(adjoint, east_a, east_b, north_a, north_b, width):
    fields, levels, columns, lanes = adjoint.shape
    chunk = 5 if levels % 5 == 0 else levels
    field_block = pl.BlockSpec((fields, chunk, columns, lanes), lambda j: (0, j, 0, 0))
    face_block = pl.BlockSpec((chunk, columns, lanes), lambda j: (j, 0, 0))
    return pl.pallas_call(
        substep_kernel,
        grid=(levels // chunk,),
        in_specs=[field_block, face_block, face_block, face_block, face_block],
        out_specs=pl.BlockSpec((fields, chunk, width, lanes), lambda j: (0, j, 0, 0)),
        out_shape=jax.ShapeDtypeStruct((fields, levels, width, lanes), jnp.float32),
    )(adjoint, east_a, east_b, north_a, north_b)


def padded_halo(pieces, width, halo, padded):
    size = lax.axis_size("grid")
    up = [(i, (i + 1) % size) for i in range(size)]
    down = [(j, i) for i, j in up]
    last = jnp.concatenate([piece[:, width - halo :] for piece in pieces], 0)
    initial = jnp.concatenate([piece[:, :halo] for piece in pieces], 0)
    before = lax.ppermute(last, "grid", up)
    after = lax.ppermute(initial, "grid", down)
    wide = []
    offset = 0
    for piece in pieces:
        rows = piece.shape[0]
        fill = jnp.zeros((rows, padded - width - 2 * halo, piece.shape[-1]), jnp.float32)
        wide.append(
            jnp.concatenate(
                [before[offset : offset + rows], piece, after[offset : offset + rows], fill], 1
            )
        )
        offset += rows
    return wide


def on_device(
    adjoint_in,
    surface_carbon,
    surface_alkalinity,
    east_velocity,
    north_velocity,
    east_diffusion,
    north_diffusion,
    vertical_mix,
    thickness,
    export_flux,
    piston,
    wet_mask,
    bottom_level,
):
    levels = vertical_mix.shape[0]
    width = east_velocity.shape[1]
    halo = SUBSTEPS
    padded = -(-(width + 2 * halo) // 8) * 8
    wet_bottom = jnp.where(wet_mask > 0, bottom_level, 0).astype(jnp.float32)
    wide_east, wide_north, wide_bottom = padded_halo(
        [east_velocity, north_velocity, wet_bottom[None]], width, halo, padded
    )
    depth_index = lax.broadcasted_iota(jnp.int32, (levels,) + wide_bottom.shape[1:], 0)
    wide_wet = (depth_index.astype(jnp.float32) < wide_bottom).astype(jnp.float32)
    wet_cube = (depth_index[:, :width] < wet_bottom[None]).astype(jnp.float32)

    below_band, diagonal, above_band = column_coefficients(vertical_mix, thickness, wet_cube)
    pivots, factors = elimination(below_band, diagonal, above_band)
    adjoint = transposed_solve(adjoint_in, below_band, pivots, factors)
    (adjoint,) = padded_halo(
        [adjoint.reshape((-1,) + adjoint.shape[-2:])], width, halo, padded
    )

    east_a, east_b = face_pairs(
        wide_east, wide_wet, jnp.roll(wide_wet, -1, axis=1), east_diffusion
    )
    zero_row = jnp.zeros(wide_wet.shape[:-1] + (1,), jnp.float32)
    north_next = jnp.concatenate([wide_wet[..., 1:], zero_row], -1)
    north_a, north_b = face_pairs(wide_north, wide_wet, north_next, north_diffusion)

    fields = adjoint_in.shape[0] * adjoint_in.shape[1]
    adjoint = transport_substeps(
        adjoint.reshape((fields, levels) + adjoint.shape[-2:]),
        east_a,
        east_b,
        north_a,
        north_b,
        width,
    ).reshape(adjoint_in.shape)
    rate_term = jnp.sum(adjoint[:, 0] - alk_ratio * adjoint[:, 1], axis=0)
    summed = scenario_sum(rate_term)
    rate_gradient = export_flux * wet_cube * summed
    slope_carbon, slope_alkalinity = carbonate_slopes(surface_carbon, surface_alkalinity)
    exchange_scale = wet_cube[0] * piston * adjoint[:, 0, 0]
    adjoint = (
        adjoint.at[:, 0, 0]
        .add(-exchange_scale * slope_carbon)
        .at[:, 1, 0]
        .add(-exchange_scale * slope_alkalinity)
    )
    return (adjoint, rate_gradient)


def solution(mesh):
    in_specs = (
        P("scen", None, None, "grid", None),
        P("scen", "grid", None),
        P("scen", "grid", None),
        P(None, "grid", None),
        P(None, "grid", None),
        P(),
        P(),
        P(None, "grid", None),
        P(),
        P(None, "grid", None),
        P("grid", None),
        P("grid", None),
        P("grid", None),
    )
    out_specs = (P("scen", None, None, "grid", None), P(None, "grid", None))
    return jax.shard_map(
        on_device, mesh=mesh, in_specs=in_specs, out_specs=out_specs, check_vma=False
    )
```

```python
import jax
import jax.numpy as jnp
from jax import lax
from jax.sharding import PartitionSpec as P
from jax.experimental import pallas as pl
from jax.experimental.pallas import tpu as pltpu

SUBSTEPS = 6


alk_ratio = 0.137


def face_pairs(velocity, mask_here, mask_next, diffusion):
    opened = mask_here * mask_next
    moving = velocity * opened
    mixing = diffusion[:, None, None] * opened
    return (mixing + jnp.maximum(moving, 0.0), jnp.minimum(moving, 0.0) - mixing)


def column_coefficients(vertical_mix, thickness, wet_cube):
    zero_layer = jnp.zeros((1,) + wet_cube.shape[1:], jnp.float32)
    opened = jnp.concatenate([wet_cube[:-1] * wet_cube[1:], zero_layer], 0)
    mixing = vertical_mix * opened
    mixing_above = jnp.concatenate([zero_layer, mixing[:-1]], 0)
    height = thickness[:, None, None]
    height_above = jnp.concatenate([thickness[:1], thickness[:-1]])[:, None, None]
    height_below = jnp.concatenate([thickness[1:], thickness[-1:]])[:, None, None]
    diagonal = 1.0 + (mixing + mixing_above) / height
    below_band = -mixing_above / height_above
    above_band = -mixing / height_below
    return (below_band, diagonal, above_band)


def solve_kernel(rhs_ref, below_ref, diagonal_ref, above_ref, out_ref, factor_ref):
    levels = diagonal_ref.shape[0]
    pivots = diagonal_ref[0]
    factor_ref[0] = above_ref[0] / pivots
    reduced = rhs_ref[:, 0] / pivots
    out_ref[:, 0] = reduced
    for level in range(1, levels):
        below = below_ref[level]
        pivots = diagonal_ref[level] - below * factor_ref[level - 1]
        factor_ref[level] = above_ref[level] / pivots
        reduced = (rhs_ref[:, level] - below * reduced) / pivots
        out_ref[:, level] = reduced
    solved = reduced
    for level in range(levels - 2, -1, -1):
        solved = out_ref[:, level] - factor_ref[level] * solved
        out_ref[:, level] = solved


def transposed_solve(right_side, below_band, diagonal, above_band):
    shape = right_side.shape
    rhs = right_side.reshape((-1,) + shape[-3:])
    out = pl.pallas_call(
        solve_kernel,
        out_shape=jax.ShapeDtypeStruct(rhs.shape, jnp.float32),
        scratch_shapes=[pltpu.VMEM(diagonal.shape, jnp.float32)],
    )(rhs, below_band, diagonal, above_band)
    return out.reshape(shape)


def carbonate_slopes(carbon, alkalinity):
    excess = 2.0 * carbon - alkalinity
    spread = alkalinity - carbon
    square = spread * spread
    return (
        (4.0 * excess * spread + excess * excess) / square,
        (-2.0 * excess * spread - excess * excess) / square,
    )


def scenario_sum(field):
    size = lax.axis_size("scen")
    index = lax.axis_index("scen")
    shape = field.shape
    rows = field.reshape(-1, shape[-1])
    bits = [b for b in (2, 4, 1) if b < size]
    bits += [b for b in (8, 16, 32) if b < size]
    kept_bits = []
    for bit in bits:
        half = rows.shape[0] // 2
        upper = (index // bit) % 2 == 1
        low, high = rows[:half], rows[half:]
        keep = jnp.where(upper, high, low)
        send = jnp.where(upper, low, high)
        pairs = [(i, i ^ bit) for i in range(size)]
        rows = keep + lax.ppermute(send, "scen", pairs)
        kept_bits.append((bit, upper))
    for bit, upper in kept_bits[::-1]:
        pairs = [(i, i ^ bit) for i in range(size)]
        other = lax.ppermute(rows, "scen", pairs)
        rows = jnp.where(
            upper,
            jnp.concatenate([other, rows], 0),
            jnp.concatenate([rows, other], 0),
        )
    return rows.reshape(shape)


def substep_kernel(adjoint_ref, east_a_ref, east_b_ref, north_a_ref, north_b_ref, out_ref):
    columns = adjoint_ref.shape[-2]
    lanes = adjoint_ref.shape[-1]
    east_a = east_a_ref[...]
    east_b_behind = pltpu.roll(east_b_ref[...], 1, 1)
    north_a = north_a_ref[...]
    north_b_behind = pltpu.roll(north_b_ref[...], 1, 2)
    for field in range(adjoint_ref.shape[0]):
        adjoint = adjoint_ref[field]
        for repeat in range(SUBSTEPS):
            ahead = pltpu.roll(adjoint, columns - 1, 1)
            behind = pltpu.roll(adjoint, 1, 1)
            north_ahead = pltpu.roll(adjoint, lanes - 1, 2)
            north_behind = pltpu.roll(adjoint, 1, 2)
            adjoint = (
                adjoint
                - east_a * (adjoint - ahead)
                - east_b_behind * (behind - adjoint)
                - (north_a * (adjoint - north_ahead) + north_b_behind * (north_behind - adjoint))
            )
        aligned = pltpu.roll(adjoint, columns - SUBSTEPS, 1)
        out_ref[field] = aligned[:, : out_ref.shape[-2]]


def transport_substeps(adjoint, east_a, east_b, north_a, north_b, width):
    fields, levels, columns, lanes = adjoint.shape
    chunk = 5 if levels % 5 == 0 else levels
    field_block = pl.BlockSpec((fields, chunk, columns, lanes), lambda j: (0, j, 0, 0))
    face_block = pl.BlockSpec((chunk, columns, lanes), lambda j: (j, 0, 0))
    return pl.pallas_call(
        substep_kernel,
        grid=(levels // chunk,),
        in_specs=[field_block, face_block, face_block, face_block, face_block],
        out_specs=pl.BlockSpec((fields, chunk, width, lanes), lambda j: (0, j, 0, 0)),
        out_shape=jax.ShapeDtypeStruct((fields, levels, width, lanes), jnp.float32),
    )(adjoint, east_a, east_b, north_a, north_b)


def padded_halo(pieces, width, halo, padded):
    size = lax.axis_size("grid")
    up = [(i, (i + 1) % size) for i in range(size)]
    down = [(j, i) for i, j in up]
    last = jnp.concatenate([piece[:, width - halo :] for piece in pieces], 0)
    initial = jnp.concatenate([piece[:, :halo] for piece in pieces], 0)
    before = lax.ppermute(last, "grid", up)
    after = lax.ppermute(initial, "grid", down)
    wide = []
    offset = 0
    for piece in pieces:
        rows = piece.shape[0]
        fill = jnp.zeros((rows, padded - width - 2 * halo, piece.shape[-1]), jnp.float32)
        wide.append(
            jnp.concatenate(
                [before[offset : offset + rows], piece, after[offset : offset + rows], fill], 1
            )
        )
        offset += rows
    return wide


def on_device(
    adjoint_in,
    surface_carbon,
    surface_alkalinity,
    east_velocity,
    north_velocity,
    east_diffusion,
    north_diffusion,
    vertical_mix,
    thickness,
    export_flux,
    piston,
    wet_mask,
    bottom_level,
):
    levels = vertical_mix.shape[0]
    width = east_velocity.shape[1]
    halo = SUBSTEPS
    padded = -(-(width + 2 * halo) // 8) * 8
    wet_bottom = jnp.where(wet_mask > 0, bottom_level, 0).astype(jnp.float32)
    wide_east, wide_north, wide_bottom = padded_halo(
        [east_velocity, north_velocity, wet_bottom[None]], width, halo, padded
    )
    depth_index = lax.broadcasted_iota(jnp.int32, (levels,) + wide_bottom.shape[1:], 0)
    wide_wet = (depth_index.astype(jnp.float32) < wide_bottom).astype(jnp.float32)
    wet_cube = (depth_index[:, :width] < wet_bottom[None]).astype(jnp.float32)

    below_band, diagonal, above_band = column_coefficients(vertical_mix, thickness, wet_cube)
    adjoint = transposed_solve(adjoint_in, below_band, diagonal, above_band)
    (adjoint,) = padded_halo(
        [adjoint.reshape((-1,) + adjoint.shape[-2:])], width, halo, padded
    )

    east_a, east_b = face_pairs(
        wide_east, wide_wet, jnp.roll(wide_wet, -1, axis=1), east_diffusion
    )
    zero_row = jnp.zeros(wide_wet.shape[:-1] + (1,), jnp.float32)
    north_next = jnp.concatenate([wide_wet[..., 1:], zero_row], -1)
    north_a, north_b = face_pairs(wide_north, wide_wet, north_next, north_diffusion)

    fields = adjoint_in.shape[0] * adjoint_in.shape[1]
    adjoint = transport_substeps(
        adjoint.reshape((fields, levels) + adjoint.shape[-2:]),
        east_a,
        east_b,
        north_a,
        north_b,
        width,
    ).reshape(adjoint_in.shape)
    rate_term = jnp.sum(adjoint[:, 0] - alk_ratio * adjoint[:, 1], axis=0)
    summed = scenario_sum(rate_term)
    rate_gradient = export_flux * wet_cube * summed
    slope_carbon, slope_alkalinity = carbonate_slopes(surface_carbon, surface_alkalinity)
    exchange_scale = wet_cube[0] * piston * adjoint[:, 0, 0]
    adjoint = (
        adjoint.at[:, 0, 0]
        .add(-exchange_scale * slope_carbon)
        .at[:, 1, 0]
        .add(-exchange_scale * slope_alkalinity)
    )
    return (adjoint, rate_gradient)


def solution(mesh):
    in_specs = (
        P("scen", None, None, "grid", None),
        P("scen", "grid", None),
        P("scen", "grid", None),
        P(None, "grid", None),
        P(None, "grid", None),
        P(),
        P(),
        P(None, "grid", None),
        P(),
        P(None, "grid", None),
        P("grid", None),
        P("grid", None),
        P("grid", None),
    )
    out_specs = (P("scen", None, None, "grid", None), P(None, "grid", None))
    return jax.shard_map(
        on_device, mesh=mesh, in_specs=in_specs, out_specs=out_specs, check_vma=False
    )
```

```python
import jax
import jax.numpy as jnp
from jax import lax
from jax.sharding import PartitionSpec as P
from jax.experimental import pallas as pl
from jax.experimental.pallas import tpu as pltpu

SUBSTEPS = 6


alk_ratio = 0.137


def face_pairs(velocity, mask_here, mask_next, diffusion):
    opened = mask_here * mask_next
    moving = velocity * opened
    mixing = diffusion[:, None, None] * opened
    return (mixing + jnp.maximum(moving, 0.0), jnp.minimum(moving, 0.0) - mixing)


def column_coefficients(vertical_mix, thickness, wet_cube):
    zero_layer = jnp.zeros((1,) + wet_cube.shape[1:], jnp.float32)
    opened = jnp.concatenate([wet_cube[:-1] * wet_cube[1:], zero_layer], 0)
    mixing = vertical_mix * opened
    mixing_above = jnp.concatenate([zero_layer, mixing[:-1]], 0)
    height = thickness[:, None, None]
    height_above = jnp.concatenate([thickness[:1], thickness[:-1]])[:, None, None]
    height_below = jnp.concatenate([thickness[1:], thickness[-1:]])[:, None, None]
    diagonal = 1.0 + (mixing + mixing_above) / height
    below_band = -mixing_above / height_above
    above_band = -mixing / height_below
    return (below_band, diagonal, above_band)


def solve_kernel(rhs_ref, below_ref, diagonal_ref, above_ref, out_ref, factor_ref):
    levels = diagonal_ref.shape[0]
    pivots = diagonal_ref[0]
    factor_ref[0] = above_ref[0] / pivots
    reduced = rhs_ref[:, 0] / pivots
    out_ref[:, 0] = reduced
    for level in range(1, levels):
        below = below_ref[level]
        pivots = diagonal_ref[level] - below * factor_ref[level - 1]
        factor_ref[level] = above_ref[level] / pivots
        reduced = (rhs_ref[:, level] - below * reduced) / pivots
        out_ref[:, level] = reduced
    solved = reduced
    for level in range(levels - 2, -1, -1):
        solved = out_ref[:, level] - factor_ref[level] * solved
        out_ref[:, level] = solved


def transposed_solve(right_side, below_band, diagonal, above_band):
    shape = right_side.shape
    rhs = right_side.reshape((-1,) + shape[-3:])
    out = pl.pallas_call(
        solve_kernel,
        out_shape=jax.ShapeDtypeStruct(rhs.shape, jnp.float32),
        scratch_shapes=[pltpu.VMEM(diagonal.shape, jnp.float32)],
    )(rhs, below_band, diagonal, above_band)
    return out.reshape(shape)


def carbonate_slopes(carbon, alkalinity):
    excess = 2.0 * carbon - alkalinity
    spread = alkalinity - carbon
    square = spread * spread
    return (
        (4.0 * excess * spread + excess * excess) / square,
        (-2.0 * excess * spread - excess * excess) / square,
    )


def scenario_rounds():
    size = lax.axis_size("scen")
    index = lax.axis_index("scen")
    bits = [b for b in (2, 4, 1) if b < size]
    bits += [b for b in (8, 16, 32) if b < size]

    def halving(bit):
        def step(rows):
            half = rows.shape[0] // 2
            upper = (index // bit) % 2 == 1
            low, high = rows[:half], rows[half:]
            keep = jnp.where(upper, high, low)
            send = jnp.where(upper, low, high)
            pairs = [(i, i ^ bit) for i in range(size)]
            return keep + lax.ppermute(send, "scen", pairs)

        return step

    def doubling(bit):
        def step(rows):
            upper = (index // bit) % 2 == 1
            pairs = [(i, i ^ bit) for i in range(size)]
            other = lax.ppermute(rows, "scen", pairs)
            return jnp.where(
                upper,
                jnp.concatenate([other, rows], 0),
                jnp.concatenate([rows, other], 0),
            )

        return step

    return [halving(bit) for bit in bits] + [doubling(bit) for bit in bits[::-1]]


def substep_kernel(adjoint_ref, east_a_ref, east_b_ref, north_a_ref, north_b_ref, out_ref):
    columns = adjoint_ref.shape[-2]
    lanes = adjoint_ref.shape[-1]
    east_a = east_a_ref[...]
    east_b_behind = pltpu.roll(east_b_ref[...], 1, 1)
    north_a = north_a_ref[...]
    north_b_behind = pltpu.roll(north_b_ref[...], 1, 2)
    for field in range(adjoint_ref.shape[0]):
        adjoint = adjoint_ref[field]
        for repeat in range(SUBSTEPS):
            ahead = pltpu.roll(adjoint, columns - 1, 1)
            behind = pltpu.roll(adjoint, 1, 1)
            north_ahead = pltpu.roll(adjoint, lanes - 1, 2)
            north_behind = pltpu.roll(adjoint, 1, 2)
            adjoint = (
                adjoint
                - east_a * (adjoint - ahead)
                - east_b_behind * (behind - adjoint)
                - (north_a * (adjoint - north_ahead) + north_b_behind * (north_behind - adjoint))
            )
        aligned = pltpu.roll(adjoint, columns - SUBSTEPS, 1)
        out_ref[field] = aligned[:, : out_ref.shape[-2]]


def transport_substeps(adjoint, east_a, east_b, north_a, north_b, width, field=0, fields=None):
    levels, columns, lanes = adjoint.shape[1:]
    fields = adjoint.shape[0] if fields is None else fields
    chunk = 5 if levels % 5 == 0 else levels
    field_block = pl.BlockSpec(
        (fields, chunk, columns, lanes), lambda j: (field // fields, j, 0, 0)
    )
    face_block = pl.BlockSpec((chunk, columns, lanes), lambda j: (j, 0, 0))
    return pl.pallas_call(
        substep_kernel,
        grid=(levels // chunk,),
        in_specs=[field_block, face_block, face_block, face_block, face_block],
        out_specs=pl.BlockSpec((fields, chunk, width, lanes), lambda j: (0, j, 0, 0)),
        out_shape=jax.ShapeDtypeStruct((fields, levels, width, lanes), jnp.float32),
    )(adjoint, east_a, east_b, north_a, north_b)


def padded_halo(pieces, width, halo, padded):
    size = lax.axis_size("grid")
    up = [(i, (i + 1) % size) for i in range(size)]
    down = [(j, i) for i, j in up]
    last = jnp.concatenate([piece[:, width - halo :] for piece in pieces], 0)
    initial = jnp.concatenate([piece[:, :halo] for piece in pieces], 0)
    before = lax.ppermute(last, "grid", up)
    after = lax.ppermute(initial, "grid", down)
    wide = []
    offset = 0
    for piece in pieces:
        rows = piece.shape[0]
        fill = jnp.zeros((rows, padded - width - 2 * halo, piece.shape[-1]), jnp.float32)
        wide.append(
            jnp.concatenate(
                [before[offset : offset + rows], piece, after[offset : offset + rows], fill], 1
            )
        )
        offset += rows
    return wide


def on_device(
    adjoint_in,
    surface_carbon,
    surface_alkalinity,
    east_velocity,
    north_velocity,
    east_diffusion,
    north_diffusion,
    vertical_mix,
    thickness,
    export_flux,
    piston,
    wet_mask,
    bottom_level,
):
    levels = vertical_mix.shape[0]
    width = east_velocity.shape[1]
    halo = SUBSTEPS
    padded = -(-(width + 2 * halo) // 8) * 8
    wet_bottom = jnp.where(wet_mask > 0, bottom_level, 0).astype(jnp.float32)
    wide_east, wide_north, wide_bottom = padded_halo(
        [east_velocity, north_velocity, wet_bottom[None]], width, halo, padded
    )
    depth_index = lax.broadcasted_iota(jnp.int32, (levels,) + wide_bottom.shape[1:], 0)
    wide_wet = (depth_index.astype(jnp.float32) < wide_bottom).astype(jnp.float32)
    wet_cube = (depth_index[:, :width] < wet_bottom[None]).astype(jnp.float32)

    rounds = scenario_rounds()
    lanes = adjoint_in.shape[-1]
    combined = jnp.sum(adjoint_in[:, 0] - alk_ratio * adjoint_in[:, 1], axis=0)
    combined = rounds[0](combined.reshape(-1, lanes))

    below_band, diagonal, above_band = column_coefficients(vertical_mix, thickness, wet_cube)
    adjoint = transposed_solve(adjoint_in, below_band, diagonal, above_band)
    combined, adjoint = lax.optimization_barrier((combined, adjoint))
    combined = rounds[1](combined)
    (adjoint,) = padded_halo(
        [adjoint.reshape((-1,) + adjoint.shape[-2:])], width, halo, padded
    )

    east_a, east_b = face_pairs(
        wide_east, wide_wet, jnp.roll(wide_wet, -1, axis=1), east_diffusion
    )
    zero_row = jnp.zeros(wide_wet.shape[:-1] + (1,), jnp.float32)
    north_next = jnp.concatenate([wide_wet[..., 1:], zero_row], -1)
    north_a, north_b = face_pairs(wide_north, wide_wet, north_next, north_diffusion)
    faces = (east_a, east_b, north_a, north_b)
    combined, adjoint, faces = lax.optimization_barrier((combined, adjoint, faces))

    fields = adjoint_in.shape[0] * adjoint_in.shape[1]
    adjoint = adjoint.reshape((fields, levels) + adjoint.shape[-2:])
    transported = []
    for field in range(fields):
        step = field + 2
        if step < len(rounds):
            combined = rounds[step](combined)
        part = transport_substeps(adjoint, *faces, width, field=field, fields=1)
        combined, part = lax.optimization_barrier((combined, part))
        transported.append(part)
    for step in range(fields + 2, len(rounds)):
        combined = rounds[step](combined)
    adjoint = jnp.concatenate(transported, 0).reshape(adjoint_in.shape)

    combined = combined.reshape((1, levels, width, lanes))
    combined = transposed_solve(combined, below_band, diagonal, above_band)
    (combined,) = padded_halo([combined[0]], width, halo, padded)
    summed = transport_substeps(combined[None], *faces, width)[0]
    rate_gradient = export_flux * wet_cube * summed
    slope_carbon, slope_alkalinity = carbonate_slopes(surface_carbon, surface_alkalinity)
    exchange_scale = wet_cube[0] * piston * adjoint[:, 0, 0]
    adjoint = (
        adjoint.at[:, 0, 0]
        .add(-exchange_scale * slope_carbon)
        .at[:, 1, 0]
        .add(-exchange_scale * slope_alkalinity)
    )
    return (adjoint, rate_gradient)


def solution(mesh):
    in_specs = (
        P("scen", None, None, "grid", None),
        P("scen", "grid", None),
        P("scen", "grid", None),
        P(None, "grid", None),
        P(None, "grid", None),
        P(),
        P(),
        P(None, "grid", None),
        P(),
        P(None, "grid", None),
        P("grid", None),
        P("grid", None),
        P("grid", None),
    )
    out_specs = (P("scen", None, None, "grid", None), P(None, "grid", None))
    return jax.shard_map(
        on_device, mesh=mesh, in_specs=in_specs, out_specs=out_specs, check_vma=False
    )
```

```python
import jax
import jax.numpy as jnp
from jax import lax
from jax.sharding import PartitionSpec as P
from jax.experimental import pallas as pl
from jax.experimental.pallas import tpu as pltpu

SUBSTEPS = 6


alk_ratio = 0.137


def face_pairs(velocity, mask_here, mask_next, diffusion):
    opened = mask_here * mask_next
    moving = velocity * opened
    mixing = diffusion[:, None, None] * opened
    return (mixing + jnp.maximum(moving, 0.0), jnp.minimum(moving, 0.0) - mixing)


def column_coefficients(vertical_mix, thickness, wet_cube):
    zero_layer = jnp.zeros((1,) + wet_cube.shape[1:], jnp.float32)
    opened = jnp.concatenate([wet_cube[:-1] * wet_cube[1:], zero_layer], 0)
    mixing = vertical_mix * opened
    mixing_above = jnp.concatenate([zero_layer, mixing[:-1]], 0)
    height = thickness[:, None, None]
    height_above = jnp.concatenate([thickness[:1], thickness[:-1]])[:, None, None]
    height_below = jnp.concatenate([thickness[1:], thickness[-1:]])[:, None, None]
    diagonal = 1.0 + (mixing + mixing_above) / height
    below_band = -mixing_above / height_above
    above_band = -mixing / height_below
    return (below_band, diagonal, above_band)


def solve_kernel(rhs_ref, below_ref, diagonal_ref, above_ref, out_ref, factor_ref):
    levels = diagonal_ref.shape[0]
    pivots = diagonal_ref[0]
    factor_ref[0] = above_ref[0] / pivots
    reduced = rhs_ref[:, 0] / pivots
    out_ref[:, 0] = reduced
    for level in range(1, levels):
        below = below_ref[level]
        pivots = diagonal_ref[level] - below * factor_ref[level - 1]
        factor_ref[level] = above_ref[level] / pivots
        reduced = (rhs_ref[:, level] - below * reduced) / pivots
        out_ref[:, level] = reduced
    solved = reduced
    for level in range(levels - 2, -1, -1):
        solved = out_ref[:, level] - factor_ref[level] * solved
        out_ref[:, level] = solved


def transposed_solve(right_side, below_band, diagonal, above_band):
    shape = right_side.shape
    rhs = right_side.reshape((-1,) + shape[-3:])
    out = pl.pallas_call(
        solve_kernel,
        out_shape=jax.ShapeDtypeStruct(rhs.shape, jnp.float32),
        scratch_shapes=[pltpu.VMEM(diagonal.shape, jnp.float32)],
    )(rhs, below_band, diagonal, above_band)
    return out.reshape(shape)


def carbonate_slopes(carbon, alkalinity):
    excess = 2.0 * carbon - alkalinity
    spread = alkalinity - carbon
    square = spread * spread
    return (
        (4.0 * excess * spread + excess * excess) / square,
        (-2.0 * excess * spread - excess * excess) / square,
    )


def scenario_sum(field):
    size = lax.axis_size("scen")
    index = lax.axis_index("scen")
    shape = field.shape
    rows = field.reshape(-1, shape[-1])
    bits = [b for b in (2, 4, 1) if b < size]
    bits += [b for b in (8, 16, 32) if b < size]
    kept_bits = []
    for bit in bits:
        half = rows.shape[0] // 2
        upper = (index // bit) % 2 == 1
        low, high = rows[:half], rows[half:]
        keep = jnp.where(upper, high, low)
        send = jnp.where(upper, low, high)
        pairs = [(i, i ^ bit) for i in range(size)]
        rows = keep + lax.ppermute(send, "scen", pairs)
        kept_bits.append((bit, upper))
    for bit, upper in kept_bits[::-1]:
        pairs = [(i, i ^ bit) for i in range(size)]
        other = lax.ppermute(rows, "scen", pairs)
        rows = jnp.where(
            upper,
            jnp.concatenate([other, rows], 0),
            jnp.concatenate([rows, other], 0),
        )
    return rows.reshape(shape)


def substep_kernel(adjoint_ref, east_a_ref, east_b_ref, north_a_ref, north_b_ref, out_ref):
    columns = adjoint_ref.shape[-2]
    lanes = adjoint_ref.shape[-1]

    def one_level(level, carry):
        east_a = east_a_ref[level]
        east_b_behind = pltpu.roll(east_b_ref[level], 1, 0)
        north_a = north_a_ref[level]
        north_b_behind = pltpu.roll(north_b_ref[level], 1, 1)
        for field in range(adjoint_ref.shape[0]):
            adjoint = adjoint_ref[field, level]
            for repeat in range(SUBSTEPS):
                ahead = pltpu.roll(adjoint, columns - 1, 0)
                behind = pltpu.roll(adjoint, 1, 0)
                north_ahead = pltpu.roll(adjoint, lanes - 1, 1)
                north_behind = pltpu.roll(adjoint, 1, 1)
                adjoint = (
                    adjoint
                    - east_a * (adjoint - ahead)
                    - east_b_behind * (behind - adjoint)
                    - (north_a * (adjoint - north_ahead) + north_b_behind * (north_behind - adjoint))
                )
            aligned = pltpu.roll(adjoint, columns - SUBSTEPS, 0)
            out_ref[field, level] = aligned[: out_ref.shape[-2]]
        return carry

    lax.fori_loop(0, adjoint_ref.shape[1], one_level, 0)


def transport_substeps(adjoint, east_a, east_b, north_a, north_b, width):
    fields, levels, columns, lanes = adjoint.shape
    chunk = 5 if levels % 5 == 0 else levels
    field_block = pl.BlockSpec((fields, chunk, columns, lanes), lambda j: (0, j, 0, 0))
    face_block = pl.BlockSpec((chunk, columns, lanes), lambda j: (j, 0, 0))
    return pl.pallas_call(
        substep_kernel,
        grid=(levels // chunk,),
        in_specs=[field_block, face_block, face_block, face_block, face_block],
        out_specs=pl.BlockSpec((fields, chunk, width, lanes), lambda j: (0, j, 0, 0)),
        out_shape=jax.ShapeDtypeStruct((fields, levels, width, lanes), jnp.float32),
    )(adjoint, east_a, east_b, north_a, north_b)


def padded_halo(pieces, width, halo, padded):
    size = lax.axis_size("grid")
    up = [(i, (i + 1) % size) for i in range(size)]
    down = [(j, i) for i, j in up]
    last = jnp.concatenate([piece[:, width - halo :] for piece in pieces], 0)
    initial = jnp.concatenate([piece[:, :halo] for piece in pieces], 0)
    before = lax.ppermute(last, "grid", up)
    after = lax.ppermute(initial, "grid", down)
    wide = []
    offset = 0
    for piece in pieces:
        rows = piece.shape[0]
        fill = jnp.zeros((rows, padded - width - 2 * halo, piece.shape[-1]), jnp.float32)
        wide.append(
            jnp.concatenate(
                [before[offset : offset + rows], piece, after[offset : offset + rows], fill], 1
            )
        )
        offset += rows
    return wide


def on_device(
    adjoint_in,
    surface_carbon,
    surface_alkalinity,
    east_velocity,
    north_velocity,
    east_diffusion,
    north_diffusion,
    vertical_mix,
    thickness,
    export_flux,
    piston,
    wet_mask,
    bottom_level,
):
    levels = vertical_mix.shape[0]
    width = east_velocity.shape[1]
    halo = SUBSTEPS
    padded = -(-(width + 2 * halo) // 8) * 8
    wet_bottom = jnp.where(wet_mask > 0, bottom_level, 0).astype(jnp.float32)
    wide_east, wide_north, wide_bottom = padded_halo(
        [east_velocity, north_velocity, wet_bottom[None]], width, halo, padded
    )
    depth_index = lax.broadcasted_iota(jnp.int32, (levels,) + wide_bottom.shape[1:], 0)
    wide_wet = (depth_index.astype(jnp.float32) < wide_bottom).astype(jnp.float32)
    wet_cube = (depth_index[:, :width] < wet_bottom[None]).astype(jnp.float32)

    below_band, diagonal, above_band = column_coefficients(vertical_mix, thickness, wet_cube)
    adjoint = transposed_solve(adjoint_in, below_band, diagonal, above_band)
    (adjoint,) = padded_halo(
        [adjoint.reshape((-1,) + adjoint.shape[-2:])], width, halo, padded
    )

    east_a, east_b = face_pairs(
        wide_east, wide_wet, jnp.roll(wide_wet, -1, axis=1), east_diffusion
    )
    zero_row = jnp.zeros(wide_wet.shape[:-1] + (1,), jnp.float32)
    north_next = jnp.concatenate([wide_wet[..., 1:], zero_row], -1)
    north_a, north_b = face_pairs(wide_north, wide_wet, north_next, north_diffusion)

    fields = adjoint_in.shape[0] * adjoint_in.shape[1]
    adjoint = transport_substeps(
        adjoint.reshape((fields, levels) + adjoint.shape[-2:]),
        east_a,
        east_b,
        north_a,
        north_b,
        width,
    ).reshape(adjoint_in.shape)
    rate_term = jnp.sum(adjoint[:, 0] - alk_ratio * adjoint[:, 1], axis=0)
    summed = scenario_sum(rate_term)
    rate_gradient = export_flux * wet_cube * summed
    slope_carbon, slope_alkalinity = carbonate_slopes(surface_carbon, surface_alkalinity)
    exchange_scale = wet_cube[0] * piston * adjoint[:, 0, 0]
    adjoint = (
        adjoint.at[:, 0, 0]
        .add(-exchange_scale * slope_carbon)
        .at[:, 1, 0]
        .add(-exchange_scale * slope_alkalinity)
    )
    return (adjoint, rate_gradient)


def solution(mesh):
    in_specs = (
        P("scen", None, None, "grid", None),
        P("scen", "grid", None),
        P("scen", "grid", None),
        P(None, "grid", None),
        P(None, "grid", None),
        P(),
        P(),
        P(None, "grid", None),
        P(),
        P(None, "grid", None),
        P("grid", None),
        P("grid", None),
        P("grid", None),
    )
    out_specs = (P("scen", None, None, "grid", None), P(None, "grid", None))
    return jax.shard_map(
        on_device, mesh=mesh, in_specs=in_specs, out_specs=out_specs, check_vma=False
    )
```

```python
import jax
import jax.numpy as jnp
from jax import lax
from jax.sharding import PartitionSpec as P
from jax.experimental import pallas as pl
from jax.experimental.pallas import tpu as pltpu

SUBSTEPS = 6


alk_ratio = 0.137


def face_pairs(velocity, mask_here, mask_next, diffusion):
    opened = mask_here * mask_next
    moving = velocity * opened
    mixing = diffusion[:, None, None] * opened
    return (mixing + jnp.maximum(moving, 0.0), jnp.minimum(moving, 0.0) - mixing)


def column_coefficients(vertical_mix, thickness, wet_cube):
    zero_layer = jnp.zeros((1,) + wet_cube.shape[1:], jnp.float32)
    opened = jnp.concatenate([wet_cube[:-1] * wet_cube[1:], zero_layer], 0)
    mixing = vertical_mix * opened
    mixing_above = jnp.concatenate([zero_layer, mixing[:-1]], 0)
    height = thickness[:, None, None]
    height_above = jnp.concatenate([thickness[:1], thickness[:-1]])[:, None, None]
    height_below = jnp.concatenate([thickness[1:], thickness[-1:]])[:, None, None]
    diagonal = 1.0 + (mixing + mixing_above) / height
    below_band = -mixing_above / height_above
    above_band = -mixing / height_below
    return (below_band, diagonal, above_band)


def solve_kernel(rhs_ref, below_ref, diagonal_ref, above_ref, out_ref, factor_ref):
    levels = diagonal_ref.shape[0]
    pivots = diagonal_ref[0]
    factor_ref[0] = above_ref[0] / pivots
    reduced = rhs_ref[:, 0] / pivots
    out_ref[:, 0] = reduced
    for level in range(1, levels):
        below = below_ref[level]
        pivots = diagonal_ref[level] - below * factor_ref[level - 1]
        factor_ref[level] = above_ref[level] / pivots
        reduced = (rhs_ref[:, level] - below * reduced) / pivots
        out_ref[:, level] = reduced
    solved = reduced
    for level in range(levels - 2, -1, -1):
        solved = out_ref[:, level] - factor_ref[level] * solved
        out_ref[:, level] = solved


def transposed_solve(right_side, below_band, diagonal, above_band):
    shape = right_side.shape
    rhs = right_side.reshape((-1,) + shape[-3:])
    out = pl.pallas_call(
        solve_kernel,
        out_shape=jax.ShapeDtypeStruct(rhs.shape, jnp.float32),
        scratch_shapes=[pltpu.VMEM(diagonal.shape, jnp.float32)],
    )(rhs, below_band, diagonal, above_band)
    return out.reshape(shape)


def carbonate_slopes(carbon, alkalinity):
    excess = 2.0 * carbon - alkalinity
    spread = alkalinity - carbon
    square = spread * spread
    return (
        (4.0 * excess * spread + excess * excess) / square,
        (-2.0 * excess * spread - excess * excess) / square,
    )


def scenario_sum(field):
    size = lax.axis_size("scen")
    index = lax.axis_index("scen")
    shape = field.shape
    rows = field.reshape(-1, shape[-1])
    bits = [b for b in (2, 4, 1) if b < size]
    bits += [b for b in (8, 16, 32) if b < size]
    kept_bits = []
    for bit in bits:
        half = rows.shape[0] // 2
        upper = (index // bit) % 2 == 1
        low, high = rows[:half], rows[half:]
        keep = jnp.where(upper, high, low)
        send = jnp.where(upper, low, high)
        pairs = [(i, i ^ bit) for i in range(size)]
        rows = keep + lax.ppermute(send, "scen", pairs)
        kept_bits.append((bit, upper))
    for bit, upper in kept_bits[::-1]:
        pairs = [(i, i ^ bit) for i in range(size)]
        other = lax.ppermute(rows, "scen", pairs)
        rows = jnp.where(
            upper,
            jnp.concatenate([other, rows], 0),
            jnp.concatenate([rows, other], 0),
        )
    return rows.reshape(shape)


def substep_kernel(adjoint_ref, east_a_ref, east_b_ref, north_a_ref, north_b_ref, out_ref):
    columns = adjoint_ref.shape[-2]
    lanes = adjoint_ref.shape[-1]
    east_a = east_a_ref[...]
    east_b_behind = pltpu.roll(east_b_ref[...], 1, 1)
    north_a = north_a_ref[...]
    north_b_behind = pltpu.roll(north_b_ref[...], 1, 2)
    for field in range(adjoint_ref.shape[0]):
        adjoint = adjoint_ref[field]
        for repeat in range(SUBSTEPS):
            ahead = pltpu.roll(adjoint, columns - 1, 1)
            behind = pltpu.roll(adjoint, 1, 1)
            north_ahead = pltpu.roll(adjoint, lanes - 1, 2)
            north_behind = pltpu.roll(adjoint, 1, 2)
            adjoint = (
                adjoint
                - east_a * (adjoint - ahead)
                - east_b_behind * (behind - adjoint)
                - (north_a * (adjoint - north_ahead) + north_b_behind * (north_behind - adjoint))
            )
        aligned = pltpu.roll(adjoint, columns - SUBSTEPS, 1)
        out_ref[field] = aligned[:, : out_ref.shape[-2]]


def transport_substeps(adjoint, east_a, east_b, north_a, north_b, width):
    fields, levels, columns, lanes = adjoint.shape
    chunk = 5 if levels % 5 == 0 else levels
    field_block = pl.BlockSpec((fields, chunk, columns, lanes), lambda j: (0, j, 0, 0))
    face_block = pl.BlockSpec((chunk, columns, lanes), lambda j: (j, 0, 0))
    return pl.pallas_call(
        substep_kernel,
        grid=(levels // chunk,),
        in_specs=[field_block, face_block, face_block, face_block, face_block],
        out_specs=pl.BlockSpec((fields, chunk, width, lanes), lambda j: (0, j, 0, 0)),
        out_shape=jax.ShapeDtypeStruct((fields, levels, width, lanes), jnp.float32),
    )(adjoint, east_a, east_b, north_a, north_b)


def padded_halo(pieces, width, halo, padded):
    size = lax.axis_size("grid")
    up = [(i, (i + 1) % size) for i in range(size)]
    down = [(j, i) for i, j in up]
    last = jnp.concatenate([piece[:, width - halo :] for piece in pieces], 0)
    initial = jnp.concatenate([piece[:, :halo] for piece in pieces], 0)
    before = lax.ppermute(last, "grid", up)
    after = lax.ppermute(initial, "grid", down)
    wide = []
    offset = 0
    for piece in pieces:
        rows = piece.shape[0]
        fill = jnp.zeros((rows, padded - width - 2 * halo, piece.shape[-1]), jnp.float32)
        wide.append(
            jnp.concatenate(
                [before[offset : offset + rows], piece, after[offset : offset + rows], fill], 1
            )
        )
        offset += rows
    return wide


def on_device(
    adjoint_in,
    surface_carbon,
    surface_alkalinity,
    east_velocity,
    north_velocity,
    east_diffusion,
    north_diffusion,
    vertical_mix,
    thickness,
    export_flux,
    piston,
    wet_mask,
    bottom_level,
):
    levels = vertical_mix.shape[0]
    width = east_velocity.shape[1]
    halo = SUBSTEPS
    padded = -(-(width + 2 * halo) // 8) * 8
    wet_bottom = jnp.where(wet_mask > 0, bottom_level, 0).astype(jnp.float32)
    wide_east, wide_north, wide_bottom = padded_halo(
        [east_velocity, north_velocity, wet_bottom[None]], width, halo, padded
    )
    depth_index = lax.broadcasted_iota(jnp.int32, (levels,) + wide_bottom.shape[1:], 0)
    wide_wet = (depth_index.astype(jnp.float32) < wide_bottom).astype(jnp.float32)
    wet_cube = (depth_index[:, :width] < wet_bottom[None]).astype(jnp.float32)

    lanes = adjoint_in.shape[-1]
    combined = jnp.sum(adjoint_in[:, 0] - alk_ratio * adjoint_in[:, 1], axis=0)
    combined = scenario_sum(combined)

    below_band, diagonal, above_band = column_coefficients(vertical_mix, thickness, wet_cube)
    adjoint = transposed_solve(adjoint_in, below_band, diagonal, above_band)
    combined = transposed_solve(combined[None], below_band, diagonal, above_band)
    fields = adjoint_in.shape[0] * adjoint_in.shape[1]
    stacked = jnp.concatenate(
        [adjoint.reshape((fields, levels, width, lanes)), combined], 0
    )
    (stacked,) = padded_halo([stacked.reshape((-1, width, lanes))], width, halo, padded)

    east_a, east_b = face_pairs(
        wide_east, wide_wet, jnp.roll(wide_wet, -1, axis=1), east_diffusion
    )
    zero_row = jnp.zeros(wide_wet.shape[:-1] + (1,), jnp.float32)
    north_next = jnp.concatenate([wide_wet[..., 1:], zero_row], -1)
    north_a, north_b = face_pairs(wide_north, wide_wet, north_next, north_diffusion)

    stacked = transport_substeps(
        stacked.reshape((fields + 1, levels, padded, lanes)),
        east_a,
        east_b,
        north_a,
        north_b,
        width,
    )
    adjoint = stacked[:fields].reshape(adjoint_in.shape)
    summed = stacked[fields]
    rate_gradient = export_flux * wet_cube * summed
    slope_carbon, slope_alkalinity = carbonate_slopes(surface_carbon, surface_alkalinity)
    exchange_scale = wet_cube[0] * piston * adjoint[:, 0, 0]
    adjoint = (
        adjoint.at[:, 0, 0]
        .add(-exchange_scale * slope_carbon)
        .at[:, 1, 0]
        .add(-exchange_scale * slope_alkalinity)
    )
    return (adjoint, rate_gradient)


def solution(mesh):
    in_specs = (
        P("scen", None, None, "grid", None),
        P("scen", "grid", None),
        P("scen", "grid", None),
        P(None, "grid", None),
        P(None, "grid", None),
        P(),
        P(),
        P(None, "grid", None),
        P(),
        P(None, "grid", None),
        P("grid", None),
        P("grid", None),
        P("grid", None),
    )
    out_specs = (P("scen", None, None, "grid", None), P(None, "grid", None))
    return jax.shard_map(
        on_device, mesh=mesh, in_specs=in_specs, out_specs=out_specs, check_vma=False
    )
```

```python
import jax
import jax.numpy as jnp
from jax import lax
from jax.sharding import PartitionSpec as P
from jax.experimental import pallas as pl
from jax.experimental.pallas import tpu as pltpu

SUBSTEPS = 6


alk_ratio = 0.137


def face_pairs(velocity, mask_here, mask_next, diffusion):
    opened = mask_here * mask_next
    moving = velocity * opened
    mixing = diffusion[:, None, None] * opened
    return (mixing + jnp.maximum(moving, 0.0), jnp.minimum(moving, 0.0) - mixing)


def column_coefficients(vertical_mix, thickness, wet_cube):
    zero_layer = jnp.zeros((1,) + wet_cube.shape[1:], jnp.float32)
    opened = jnp.concatenate([wet_cube[:-1] * wet_cube[1:], zero_layer], 0)
    mixing = vertical_mix * opened
    mixing_above = jnp.concatenate([zero_layer, mixing[:-1]], 0)
    height = thickness[:, None, None]
    height_above = jnp.concatenate([thickness[:1], thickness[:-1]])[:, None, None]
    height_below = jnp.concatenate([thickness[1:], thickness[-1:]])[:, None, None]
    diagonal = 1.0 + (mixing + mixing_above) / height
    below_band = -mixing_above / height_above
    above_band = -mixing / height_below
    return (below_band, diagonal, above_band)


def solve_kernel(rhs_ref, below_ref, diagonal_ref, above_ref, out_ref, factor_ref):
    levels = diagonal_ref.shape[0]
    pivots = diagonal_ref[0]
    factor_ref[0] = above_ref[0] / pivots
    reduced = rhs_ref[:, 0] / pivots
    out_ref[:, 0] = reduced
    for level in range(1, levels):
        below = below_ref[level]
        pivots = diagonal_ref[level] - below * factor_ref[level - 1]
        factor_ref[level] = above_ref[level] / pivots
        reduced = (rhs_ref[:, level] - below * reduced) / pivots
        out_ref[:, level] = reduced
    solved = reduced
    for level in range(levels - 2, -1, -1):
        solved = out_ref[:, level] - factor_ref[level] * solved
        out_ref[:, level] = solved


def transposed_solve(right_side, below_band, diagonal, above_band):
    shape = right_side.shape
    rhs = right_side.reshape((-1,) + shape[-3:])
    out = pl.pallas_call(
        solve_kernel,
        out_shape=jax.ShapeDtypeStruct(rhs.shape, jnp.float32),
        scratch_shapes=[pltpu.VMEM(diagonal.shape, jnp.float32)],
    )(rhs, below_band, diagonal, above_band)
    return out.reshape(shape)


def carbonate_slopes(carbon, alkalinity):
    excess = 2.0 * carbon - alkalinity
    spread = alkalinity - carbon
    square = spread * spread
    return (
        (4.0 * excess * spread + excess * excess) / square,
        (-2.0 * excess * spread - excess * excess) / square,
    )


def scenario_sum(field):
    size = lax.axis_size("scen")
    index = lax.axis_index("scen")
    shape = field.shape
    rows = field.reshape(-1, shape[-1])
    bits = [b for b in (2, 4, 1) if b < size]
    bits += [b for b in (8, 16, 32) if b < size]
    kept_bits = []
    for bit in bits:
        half = rows.shape[0] // 2
        upper = (index // bit) % 2 == 1
        low, high = rows[:half], rows[half:]
        keep = jnp.where(upper, high, low)
        send = jnp.where(upper, low, high)
        pairs = [(i, i ^ bit) for i in range(size)]
        rows = keep + lax.ppermute(send, "scen", pairs)
        kept_bits.append((bit, upper))
    for bit, upper in kept_bits[::-1]:
        pairs = [(i, i ^ bit) for i in range(size)]
        other = lax.ppermute(rows, "scen", pairs)
        rows = jnp.where(
            upper,
            jnp.concatenate([other, rows], 0),
            jnp.concatenate([rows, other], 0),
        )
    return rows.reshape(shape)


def substep_kernel(*refs):
    count = (len(refs) - 4) // 2
    field_refs, faces, out_refs = refs[:count], refs[count : count + 4], refs[count + 4 :]
    east_a_ref, east_b_ref, north_a_ref, north_b_ref = faces
    columns = field_refs[0].shape[-2]
    lanes = field_refs[0].shape[-1]
    east_a = east_a_ref[...]
    east_b_behind = pltpu.roll(east_b_ref[...], 1, 1)
    north_a = north_a_ref[...]
    north_b_behind = pltpu.roll(north_b_ref[...], 1, 2)
    for adjoint_ref, out_ref in zip(field_refs, out_refs):
        for field in range(adjoint_ref.shape[0]):
            adjoint = adjoint_ref[field]
            for repeat in range(SUBSTEPS):
                ahead = pltpu.roll(adjoint, columns - 1, 1)
                behind = pltpu.roll(adjoint, 1, 1)
                north_ahead = pltpu.roll(adjoint, lanes - 1, 2)
                north_behind = pltpu.roll(adjoint, 1, 2)
                adjoint = (
                    adjoint
                    - east_a * (adjoint - ahead)
                    - east_b_behind * (behind - adjoint)
                    - (north_a * (adjoint - north_ahead) + north_b_behind * (north_behind - adjoint))
                )
            aligned = pltpu.roll(adjoint, columns - SUBSTEPS, 1)
            out_ref[field] = aligned[:, : out_ref.shape[-2]]


def transport_substeps(adjoints, east_a, east_b, north_a, north_b, width):
    levels, columns, lanes = adjoints[0].shape[1:]
    chunk = 5 if levels % 5 == 0 else levels
    face_block = pl.BlockSpec((chunk, columns, lanes), lambda j: (j, 0, 0))
    in_blocks = [
        pl.BlockSpec((a.shape[0], chunk, columns, lanes), lambda j: (0, j, 0, 0)) for a in adjoints
    ]
    out_blocks = [
        pl.BlockSpec((a.shape[0], chunk, width, lanes), lambda j: (0, j, 0, 0)) for a in adjoints
    ]
    return pl.pallas_call(
        substep_kernel,
        grid=(levels // chunk,),
        in_specs=in_blocks + [face_block] * 4,
        out_specs=out_blocks,
        out_shape=[
            jax.ShapeDtypeStruct((a.shape[0], levels, width, lanes), jnp.float32) for a in adjoints
        ],
    )(*adjoints, east_a, east_b, north_a, north_b)


def padded_halo(pieces, width, halo, padded):
    size = lax.axis_size("grid")
    up = [(i, (i + 1) % size) for i in range(size)]
    down = [(j, i) for i, j in up]
    last = jnp.concatenate([piece[:, width - halo :] for piece in pieces], 0)
    initial = jnp.concatenate([piece[:, :halo] for piece in pieces], 0)
    before = lax.ppermute(last, "grid", up)
    after = lax.ppermute(initial, "grid", down)
    wide = []
    offset = 0
    for piece in pieces:
        rows = piece.shape[0]
        fill = jnp.zeros((rows, padded - width - 2 * halo, piece.shape[-1]), jnp.float32)
        wide.append(
            jnp.concatenate(
                [before[offset : offset + rows], piece, after[offset : offset + rows], fill], 1
            )
        )
        offset += rows
    return wide


def on_device(
    adjoint_in,
    surface_carbon,
    surface_alkalinity,
    east_velocity,
    north_velocity,
    east_diffusion,
    north_diffusion,
    vertical_mix,
    thickness,
    export_flux,
    piston,
    wet_mask,
    bottom_level,
):
    levels = vertical_mix.shape[0]
    width = east_velocity.shape[1]
    halo = SUBSTEPS
    padded = -(-(width + 2 * halo) // 8) * 8
    wet_bottom = jnp.where(wet_mask > 0, bottom_level, 0).astype(jnp.float32)
    wide_east, wide_north, wide_bottom = padded_halo(
        [east_velocity, north_velocity, wet_bottom[None]], width, halo, padded
    )
    depth_index = lax.broadcasted_iota(jnp.int32, (levels,) + wide_bottom.shape[1:], 0)
    wide_wet = (depth_index.astype(jnp.float32) < wide_bottom).astype(jnp.float32)
    wet_cube = (depth_index[:, :width] < wet_bottom[None]).astype(jnp.float32)

    lanes = adjoint_in.shape[-1]
    combined = jnp.sum(adjoint_in[:, 0] - alk_ratio * adjoint_in[:, 1], axis=0)
    combined = scenario_sum(combined)

    below_band, diagonal, above_band = column_coefficients(vertical_mix, thickness, wet_cube)
    adjoint = transposed_solve(adjoint_in, below_band, diagonal, above_band)
    fields = adjoint_in.shape[0] * adjoint_in.shape[1]
    (adjoint,) = padded_halo([adjoint.reshape((-1, width, lanes))], width, halo, padded)
    combined = transposed_solve(combined[None], below_band, diagonal, above_band)
    (combined,) = padded_halo([combined[0]], width, halo, padded)

    east_a, east_b = face_pairs(
        wide_east, wide_wet, jnp.roll(wide_wet, -1, axis=1), east_diffusion
    )
    zero_row = jnp.zeros(wide_wet.shape[:-1] + (1,), jnp.float32)
    north_next = jnp.concatenate([wide_wet[..., 1:], zero_row], -1)
    north_a, north_b = face_pairs(wide_north, wide_wet, north_next, north_diffusion)

    adjoint, summed = transport_substeps(
        [adjoint.reshape((fields, levels, padded, lanes)), combined[None]],
        east_a,
        east_b,
        north_a,
        north_b,
        width,
    )
    adjoint = adjoint.reshape(adjoint_in.shape)
    summed = summed[0]
    rate_gradient = export_flux * wet_cube * summed
    slope_carbon, slope_alkalinity = carbonate_slopes(surface_carbon, surface_alkalinity)
    exchange_scale = wet_cube[0] * piston * adjoint[:, 0, 0]
    adjoint = (
        adjoint.at[:, 0, 0]
        .add(-exchange_scale * slope_carbon)
        .at[:, 1, 0]
        .add(-exchange_scale * slope_alkalinity)
    )
    return (adjoint, rate_gradient)


def solution(mesh):
    in_specs = (
        P("scen", None, None, "grid", None),
        P("scen", "grid", None),
        P("scen", "grid", None),
        P(None, "grid", None),
        P(None, "grid", None),
        P(),
        P(),
        P(None, "grid", None),
        P(),
        P(None, "grid", None),
        P("grid", None),
        P("grid", None),
        P("grid", None),
    )
    out_specs = (P("scen", None, None, "grid", None), P(None, "grid", None))
    return jax.shard_map(
        on_device, mesh=mesh, in_specs=in_specs, out_specs=out_specs, check_vma=False
    )
```

```python
import jax
import jax.numpy as jnp
from jax import lax
from jax.sharding import PartitionSpec as P
from jax.experimental import pallas as pl
from jax.experimental.pallas import tpu as pltpu

SUBSTEPS = 6


alk_ratio = 0.137


def face_pairs(velocity, mask_here, mask_next, diffusion):
    opened = mask_here * mask_next
    moving = velocity * opened
    mixing = diffusion[:, None, None] * opened
    return (mixing + jnp.maximum(moving, 0.0), jnp.minimum(moving, 0.0) - mixing)


def column_coefficients(vertical_mix, thickness, wet_cube):
    zero_layer = jnp.zeros((1,) + wet_cube.shape[1:], jnp.float32)
    opened = jnp.concatenate([wet_cube[:-1] * wet_cube[1:], zero_layer], 0)
    mixing = vertical_mix * opened
    mixing_above = jnp.concatenate([zero_layer, mixing[:-1]], 0)
    height = thickness[:, None, None]
    height_above = jnp.concatenate([thickness[:1], thickness[:-1]])[:, None, None]
    height_below = jnp.concatenate([thickness[1:], thickness[-1:]])[:, None, None]
    diagonal = 1.0 + (mixing + mixing_above) / height
    below_band = -mixing_above / height_above
    above_band = -mixing / height_below
    return (below_band, diagonal, above_band)


def solve_kernel(rhs_ref, below_ref, diagonal_ref, above_ref, out_ref, factor_ref):
    levels = diagonal_ref.shape[0]
    pivots = diagonal_ref[0]
    factor_ref[0] = above_ref[0] / pivots
    reduced = rhs_ref[:, 0] / pivots
    out_ref[:, 0] = reduced
    for level in range(1, levels):
        below = below_ref[level]
        pivots = diagonal_ref[level] - below * factor_ref[level - 1]
        factor_ref[level] = above_ref[level] / pivots
        reduced = (rhs_ref[:, level] - below * reduced) / pivots
        out_ref[:, level] = reduced
    solved = reduced
    for level in range(levels - 2, -1, -1):
        solved = out_ref[:, level] - factor_ref[level] * solved
        out_ref[:, level] = solved


def transposed_solve(right_side, below_band, diagonal, above_band):
    shape = right_side.shape
    rhs = right_side.reshape((-1,) + shape[-3:])
    out = pl.pallas_call(
        solve_kernel,
        out_shape=jax.ShapeDtypeStruct(rhs.shape, jnp.float32),
        scratch_shapes=[pltpu.VMEM(diagonal.shape, jnp.float32)],
    )(rhs, below_band, diagonal, above_band)
    return out.reshape(shape)


def carbonate_slopes(carbon, alkalinity):
    excess = 2.0 * carbon - alkalinity
    spread = alkalinity - carbon
    square = spread * spread
    return (
        (4.0 * excess * spread + excess * excess) / square,
        (-2.0 * excess * spread - excess * excess) / square,
    )


def scenario_sum(field):
    size = lax.axis_size("scen")
    index = lax.axis_index("scen")
    shape = field.shape
    rows = field.reshape(-1, shape[-1])
    bits = [b for b in (2, 4, 1) if b < size]
    bits += [b for b in (8, 16, 32) if b < size]
    kept_bits = []
    for bit in bits:
        half = rows.shape[0] // 2
        upper = (index // bit) % 2 == 1
        low, high = rows[:half], rows[half:]
        keep = jnp.where(upper, high, low)
        send = jnp.where(upper, low, high)
        pairs = [(i, i ^ bit) for i in range(size)]
        rows = keep + lax.ppermute(send, "scen", pairs)
        kept_bits.append((bit, upper))
    for bit, upper in kept_bits[::-1]:
        pairs = [(i, i ^ bit) for i in range(size)]
        other = lax.ppermute(rows, "scen", pairs)
        rows = jnp.where(
            upper,
            jnp.concatenate([other, rows], 0),
            jnp.concatenate([rows, other], 0),
        )
    return rows.reshape(shape)


def substep_kernel(adjoint_ref, east_a_ref, east_b_ref, north_a_ref, north_b_ref, out_ref):
    columns = adjoint_ref.shape[-2]
    lanes = adjoint_ref.shape[-1]
    east_a = east_a_ref[...]
    east_b_behind = pltpu.roll(east_b_ref[...], 1, 1)
    north_a = north_a_ref[...]
    north_b_behind = pltpu.roll(north_b_ref[...], 1, 2)
    centre = 1.0 - east_a + east_b_behind - north_a + north_b_behind
    for field in range(adjoint_ref.shape[0]):
        adjoint = adjoint_ref[field]
        for repeat in range(SUBSTEPS):
            ahead = pltpu.roll(adjoint, columns - 1, 1)
            behind = pltpu.roll(adjoint, 1, 1)
            north_ahead = pltpu.roll(adjoint, lanes - 1, 2)
            north_behind = pltpu.roll(adjoint, 1, 2)
            adjoint = (
                centre * adjoint
                + east_a * ahead
                - east_b_behind * behind
                + north_a * north_ahead
                - north_b_behind * north_behind
            )
        aligned = pltpu.roll(adjoint, columns - SUBSTEPS, 1)
        out_ref[field] = aligned[:, : out_ref.shape[-2]]


def transport_substeps(adjoint, east_a, east_b, north_a, north_b, width):
    fields, levels, columns, lanes = adjoint.shape
    chunk = 5 if levels % 5 == 0 else levels
    field_block = pl.BlockSpec((fields, chunk, columns, lanes), lambda j: (0, j, 0, 0))
    face_block = pl.BlockSpec((chunk, columns, lanes), lambda j: (j, 0, 0))
    return pl.pallas_call(
        substep_kernel,
        grid=(levels // chunk,),
        in_specs=[field_block, face_block, face_block, face_block, face_block],
        out_specs=pl.BlockSpec((fields, chunk, width, lanes), lambda j: (0, j, 0, 0)),
        out_shape=jax.ShapeDtypeStruct((fields, levels, width, lanes), jnp.float32),
    )(adjoint, east_a, east_b, north_a, north_b)


def padded_halo(pieces, width, halo, padded):
    size = lax.axis_size("grid")
    up = [(i, (i + 1) % size) for i in range(size)]
    down = [(j, i) for i, j in up]
    last = jnp.concatenate([piece[:, width - halo :] for piece in pieces], 0)
    initial = jnp.concatenate([piece[:, :halo] for piece in pieces], 0)
    before = lax.ppermute(last, "grid", up)
    after = lax.ppermute(initial, "grid", down)
    wide = []
    offset = 0
    for piece in pieces:
        rows = piece.shape[0]
        fill = jnp.zeros((rows, padded - width - 2 * halo, piece.shape[-1]), jnp.float32)
        wide.append(
            jnp.concatenate(
                [before[offset : offset + rows], piece, after[offset : offset + rows], fill], 1
            )
        )
        offset += rows
    return wide


def on_device(
    adjoint_in,
    surface_carbon,
    surface_alkalinity,
    east_velocity,
    north_velocity,
    east_diffusion,
    north_diffusion,
    vertical_mix,
    thickness,
    export_flux,
    piston,
    wet_mask,
    bottom_level,
):
    levels = vertical_mix.shape[0]
    width = east_velocity.shape[1]
    halo = SUBSTEPS
    padded = -(-(width + 2 * halo) // 8) * 8
    wet_bottom = jnp.where(wet_mask > 0, bottom_level, 0).astype(jnp.float32)
    wide_east, wide_north, wide_bottom = padded_halo(
        [east_velocity, north_velocity, wet_bottom[None]], width, halo, padded
    )
    depth_index = lax.broadcasted_iota(jnp.int32, (levels,) + wide_bottom.shape[1:], 0)
    wide_wet = (depth_index.astype(jnp.float32) < wide_bottom).astype(jnp.float32)
    wet_cube = (depth_index[:, :width] < wet_bottom[None]).astype(jnp.float32)

    below_band, diagonal, above_band = column_coefficients(vertical_mix, thickness, wet_cube)
    adjoint = transposed_solve(adjoint_in, below_band, diagonal, above_band)
    (adjoint,) = padded_halo(
        [adjoint.reshape((-1,) + adjoint.shape[-2:])], width, halo, padded
    )

    east_a, east_b = face_pairs(
        wide_east, wide_wet, jnp.roll(wide_wet, -1, axis=1), east_diffusion
    )
    zero_row = jnp.zeros(wide_wet.shape[:-1] + (1,), jnp.float32)
    north_next = jnp.concatenate([wide_wet[..., 1:], zero_row], -1)
    north_a, north_b = face_pairs(wide_north, wide_wet, north_next, north_diffusion)

    fields = adjoint_in.shape[0] * adjoint_in.shape[1]
    adjoint = transport_substeps(
        adjoint.reshape((fields, levels) + adjoint.shape[-2:]),
        east_a,
        east_b,
        north_a,
        north_b,
        width,
    ).reshape(adjoint_in.shape)
    rate_term = jnp.sum(adjoint[:, 0] - alk_ratio * adjoint[:, 1], axis=0)
    summed = scenario_sum(rate_term)
    rate_gradient = export_flux * wet_cube * summed
    slope_carbon, slope_alkalinity = carbonate_slopes(surface_carbon, surface_alkalinity)
    exchange_scale = wet_cube[0] * piston * adjoint[:, 0, 0]
    adjoint = (
        adjoint.at[:, 0, 0]
        .add(-exchange_scale * slope_carbon)
        .at[:, 1, 0]
        .add(-exchange_scale * slope_alkalinity)
    )
    return (adjoint, rate_gradient)


def solution(mesh):
    in_specs = (
        P("scen", None, None, "grid", None),
        P("scen", "grid", None),
        P("scen", "grid", None),
        P(None, "grid", None),
        P(None, "grid", None),
        P(),
        P(),
        P(None, "grid", None),
        P(),
        P(None, "grid", None),
        P("grid", None),
        P("grid", None),
        P("grid", None),
    )
    out_specs = (P("scen", None, None, "grid", None), P(None, "grid", None))
    return jax.shard_map(
        on_device, mesh=mesh, in_specs=in_specs, out_specs=out_specs, check_vma=False
    )
```

```python
import jax
import jax.numpy as jnp
from jax import lax
from jax.sharding import PartitionSpec as P
from jax.experimental import pallas as pl
from jax.experimental.pallas import tpu as pltpu

SUBSTEPS = 6


alk_ratio = 0.137


def face_pairs(velocity, mask_here, mask_next, diffusion):
    opened = mask_here * mask_next
    moving = velocity * opened
    mixing = diffusion[:, None, None] * opened
    return (mixing + jnp.maximum(moving, 0.0), jnp.minimum(moving, 0.0) - mixing)


def column_coefficients(vertical_mix, thickness, wet_cube):
    zero_layer = jnp.zeros((1,) + wet_cube.shape[1:], jnp.float32)
    opened = jnp.concatenate([wet_cube[:-1] * wet_cube[1:], zero_layer], 0)
    mixing = vertical_mix * opened
    mixing_above = jnp.concatenate([zero_layer, mixing[:-1]], 0)
    height = thickness[:, None, None]
    height_above = jnp.concatenate([thickness[:1], thickness[:-1]])[:, None, None]
    height_below = jnp.concatenate([thickness[1:], thickness[-1:]])[:, None, None]
    diagonal = 1.0 + (mixing + mixing_above) / height
    below_band = -mixing_above / height_above
    above_band = -mixing / height_below
    return (below_band, diagonal, above_band)


def solve_kernel(rhs_ref, below_ref, diagonal_ref, above_ref, out_ref, factor_ref):
    levels = diagonal_ref.shape[0]
    pivots = diagonal_ref[0]
    factor_ref[0] = above_ref[0] / pivots
    reduced = rhs_ref[:, 0] / pivots
    out_ref[:, 0] = reduced
    for level in range(1, levels):
        below = below_ref[level]
        pivots = diagonal_ref[level] - below * factor_ref[level - 1]
        factor_ref[level] = above_ref[level] / pivots
        reduced = (rhs_ref[:, level] - below * reduced) / pivots
        out_ref[:, level] = reduced
    solved = reduced
    for level in range(levels - 2, -1, -1):
        solved = out_ref[:, level] - factor_ref[level] * solved
        out_ref[:, level] = solved


def transposed_solve(right_side, below_band, diagonal, above_band):
    shape = right_side.shape
    rhs = right_side.reshape((-1,) + shape[-3:])
    out = pl.pallas_call(
        solve_kernel,
        out_shape=jax.ShapeDtypeStruct(rhs.shape, jnp.float32),
        scratch_shapes=[pltpu.VMEM(diagonal.shape, jnp.float32)],
    )(rhs, below_band, diagonal, above_band)
    return out.reshape(shape)


def carbonate_slopes(carbon, alkalinity):
    excess = 2.0 * carbon - alkalinity
    spread = alkalinity - carbon
    square = spread * spread
    return (
        (4.0 * excess * spread + excess * excess) / square,
        (-2.0 * excess * spread - excess * excess) / square,
    )


def scenario_sum(field):
    size = lax.axis_size("scen")
    shape = field.shape
    pieces = field.reshape((size, -1, shape[-1]))
    gathered = lax.all_to_all(pieces, "scen", 0, 0, tiled=True)
    owned = jnp.sum(gathered, axis=0)
    spread = jnp.broadcast_to(owned[None], (size,) + owned.shape)
    return lax.all_to_all(spread, "scen", 0, 0, tiled=True).reshape(shape)


def substep_kernel(adjoint_ref, east_a_ref, east_b_ref, north_a_ref, north_b_ref, out_ref):
    columns = adjoint_ref.shape[-2]
    lanes = adjoint_ref.shape[-1]
    east_a = east_a_ref[...]
    east_b_behind = pltpu.roll(east_b_ref[...], 1, 1)
    north_a = north_a_ref[...]
    north_b_behind = pltpu.roll(north_b_ref[...], 1, 2)
    for field in range(adjoint_ref.shape[0]):
        adjoint = adjoint_ref[field]
        for repeat in range(SUBSTEPS):
            ahead = pltpu.roll(adjoint, columns - 1, 1)
            behind = pltpu.roll(adjoint, 1, 1)
            north_ahead = pltpu.roll(adjoint, lanes - 1, 2)
            north_behind = pltpu.roll(adjoint, 1, 2)
            adjoint = (
                adjoint
                - east_a * (adjoint - ahead)
                - east_b_behind * (behind - adjoint)
                - (north_a * (adjoint - north_ahead) + north_b_behind * (north_behind - adjoint))
            )
        aligned = pltpu.roll(adjoint, columns - SUBSTEPS, 1)
        out_ref[field] = aligned[:, : out_ref.shape[-2]]


def transport_substeps(adjoint, east_a, east_b, north_a, north_b, width):
    fields, levels, columns, lanes = adjoint.shape
    chunk = 5 if levels % 5 == 0 else levels
    field_block = pl.BlockSpec((fields, chunk, columns, lanes), lambda j: (0, j, 0, 0))
    face_block = pl.BlockSpec((chunk, columns, lanes), lambda j: (j, 0, 0))
    return pl.pallas_call(
        substep_kernel,
        grid=(levels // chunk,),
        in_specs=[field_block, face_block, face_block, face_block, face_block],
        out_specs=pl.BlockSpec((fields, chunk, width, lanes), lambda j: (0, j, 0, 0)),
        out_shape=jax.ShapeDtypeStruct((fields, levels, width, lanes), jnp.float32),
    )(adjoint, east_a, east_b, north_a, north_b)


def padded_halo(pieces, width, halo, padded):
    size = lax.axis_size("grid")
    up = [(i, (i + 1) % size) for i in range(size)]
    down = [(j, i) for i, j in up]
    last = jnp.concatenate([piece[:, width - halo :] for piece in pieces], 0)
    initial = jnp.concatenate([piece[:, :halo] for piece in pieces], 0)
    before = lax.ppermute(last, "grid", up)
    after = lax.ppermute(initial, "grid", down)
    wide = []
    offset = 0
    for piece in pieces:
        rows = piece.shape[0]
        fill = jnp.zeros((rows, padded - width - 2 * halo, piece.shape[-1]), jnp.float32)
        wide.append(
            jnp.concatenate(
                [before[offset : offset + rows], piece, after[offset : offset + rows], fill], 1
            )
        )
        offset += rows
    return wide


def on_device(
    adjoint_in,
    surface_carbon,
    surface_alkalinity,
    east_velocity,
    north_velocity,
    east_diffusion,
    north_diffusion,
    vertical_mix,
    thickness,
    export_flux,
    piston,
    wet_mask,
    bottom_level,
):
    levels = vertical_mix.shape[0]
    width = east_velocity.shape[1]
    halo = SUBSTEPS
    padded = -(-(width + 2 * halo) // 8) * 8
    wet_bottom = jnp.where(wet_mask > 0, bottom_level, 0).astype(jnp.float32)
    wide_east, wide_north, wide_bottom = padded_halo(
        [east_velocity, north_velocity, wet_bottom[None]], width, halo, padded
    )
    depth_index = lax.broadcasted_iota(jnp.int32, (levels,) + wide_bottom.shape[1:], 0)
    wide_wet = (depth_index.astype(jnp.float32) < wide_bottom).astype(jnp.float32)
    wet_cube = (depth_index[:, :width] < wet_bottom[None]).astype(jnp.float32)

    below_band, diagonal, above_band = column_coefficients(vertical_mix, thickness, wet_cube)
    adjoint = transposed_solve(adjoint_in, below_band, diagonal, above_band)
    (adjoint,) = padded_halo(
        [adjoint.reshape((-1,) + adjoint.shape[-2:])], width, halo, padded
    )

    east_a, east_b = face_pairs(
        wide_east, wide_wet, jnp.roll(wide_wet, -1, axis=1), east_diffusion
    )
    zero_row = jnp.zeros(wide_wet.shape[:-1] + (1,), jnp.float32)
    north_next = jnp.concatenate([wide_wet[..., 1:], zero_row], -1)
    north_a, north_b = face_pairs(wide_north, wide_wet, north_next, north_diffusion)

    fields = adjoint_in.shape[0] * adjoint_in.shape[1]
    adjoint = transport_substeps(
        adjoint.reshape((fields, levels) + adjoint.shape[-2:]),
        east_a,
        east_b,
        north_a,
        north_b,
        width,
    ).reshape(adjoint_in.shape)
    rate_term = jnp.sum(adjoint[:, 0] - alk_ratio * adjoint[:, 1], axis=0)
    summed = scenario_sum(rate_term)
    rate_gradient = export_flux * wet_cube * summed
    slope_carbon, slope_alkalinity = carbonate_slopes(surface_carbon, surface_alkalinity)
    exchange_scale = wet_cube[0] * piston * adjoint[:, 0, 0]
    adjoint = (
        adjoint.at[:, 0, 0]
        .add(-exchange_scale * slope_carbon)
        .at[:, 1, 0]
        .add(-exchange_scale * slope_alkalinity)
    )
    return (adjoint, rate_gradient)


def solution(mesh):
    in_specs = (
        P("scen", None, None, "grid", None),
        P("scen", "grid", None),
        P("scen", "grid", None),
        P(None, "grid", None),
        P(None, "grid", None),
        P(),
        P(),
        P(None, "grid", None),
        P(),
        P(None, "grid", None),
        P("grid", None),
        P("grid", None),
        P("grid", None),
    )
    out_specs = (P("scen", None, None, "grid", None), P(None, "grid", None))
    return jax.shard_map(
        on_device, mesh=mesh, in_specs=in_specs, out_specs=out_specs, check_vma=False
    )
```

```python
import jax
import jax.numpy as jnp
from jax import lax
from jax.sharding import PartitionSpec as P
from jax.experimental import pallas as pl
from jax.experimental.pallas import tpu as pltpu

SUBSTEPS = 6


alk_ratio = 0.137


def face_pairs(velocity, mask_here, mask_next, diffusion):
    opened = mask_here * mask_next
    moving = velocity * opened
    mixing = diffusion[:, None, None] * opened
    return (mixing + jnp.maximum(moving, 0.0), jnp.minimum(moving, 0.0) - mixing)


def column_coefficients(vertical_mix, thickness, wet_cube):
    zero_layer = jnp.zeros((1,) + wet_cube.shape[1:], jnp.float32)
    opened = jnp.concatenate([wet_cube[:-1] * wet_cube[1:], zero_layer], 0)
    mixing = vertical_mix * opened
    mixing_above = jnp.concatenate([zero_layer, mixing[:-1]], 0)
    height = thickness[:, None, None]
    height_above = jnp.concatenate([thickness[:1], thickness[:-1]])[:, None, None]
    height_below = jnp.concatenate([thickness[1:], thickness[-1:]])[:, None, None]
    diagonal = 1.0 + (mixing + mixing_above) / height
    below_band = -mixing_above / height_above
    above_band = -mixing / height_below
    return (below_band, diagonal, above_band)


def solve_kernel(rhs_ref, below_ref, diagonal_ref, above_ref, out_ref, factor_ref):
    levels = diagonal_ref.shape[0]
    pivots = diagonal_ref[0]
    factor_ref[0] = above_ref[0] / pivots
    reduced = rhs_ref[:, 0] / pivots
    out_ref[:, 0] = reduced
    for level in range(1, levels):
        below = below_ref[level]
        pivots = diagonal_ref[level] - below * factor_ref[level - 1]
        factor_ref[level] = above_ref[level] / pivots
        reduced = (rhs_ref[:, level] - below * reduced) / pivots
        out_ref[:, level] = reduced
    solved = reduced
    for level in range(levels - 2, -1, -1):
        solved = out_ref[:, level] - factor_ref[level] * solved
        out_ref[:, level] = solved


def transposed_solve(right_side, below_band, diagonal, above_band):
    shape = right_side.shape
    rhs = right_side.reshape((-1,) + shape[-3:])
    out = pl.pallas_call(
        solve_kernel,
        out_shape=jax.ShapeDtypeStruct(rhs.shape, jnp.float32),
        scratch_shapes=[pltpu.VMEM(diagonal.shape, jnp.float32)],
    )(rhs, below_band, diagonal, above_band)
    return out.reshape(shape)


def carbonate_slopes(carbon, alkalinity):
    excess = 2.0 * carbon - alkalinity
    spread = alkalinity - carbon
    square = spread * spread
    return (
        (4.0 * excess * spread + excess * excess) / square,
        (-2.0 * excess * spread - excess * excess) / square,
    )


def scenario_sum(field):
    size = lax.axis_size("scen")
    shape = field.shape
    pieces = field.reshape((size, -1, shape[-1]))
    gathered = lax.all_to_all(pieces, "scen", 0, 0, tiled=True)
    owned = jnp.sum(gathered, axis=0)
    spread = jnp.broadcast_to(owned[None], (size,) + owned.shape)
    return lax.all_to_all(spread, "scen", 0, 0, tiled=True).reshape(shape)


def substep_kernel(adjoint_ref, east_a_ref, east_b_ref, north_a_ref, north_b_ref, out_ref):
    columns = adjoint_ref.shape[-2]
    lanes = adjoint_ref.shape[-1]
    east_a = east_a_ref[...]
    east_b_behind = pltpu.roll(east_b_ref[...], 1, 1)
    north_a = north_a_ref[...]
    north_b_behind = pltpu.roll(north_b_ref[...], 1, 2)
    for field in range(adjoint_ref.shape[0]):
        adjoint = adjoint_ref[field]
        for repeat in range(SUBSTEPS):
            ahead = pltpu.roll(adjoint, columns - 1, 1)
            behind = pltpu.roll(adjoint, 1, 1)
            north_ahead = pltpu.roll(adjoint, lanes - 1, 2)
            north_behind = pltpu.roll(adjoint, 1, 2)
            adjoint = (
                adjoint
                - east_a * (adjoint - ahead)
                - east_b_behind * (behind - adjoint)
                - (north_a * (adjoint - north_ahead) + north_b_behind * (north_behind - adjoint))
            )
        aligned = pltpu.roll(adjoint, columns - SUBSTEPS, 1)
        out_ref[field] = aligned[:, : out_ref.shape[-2]]


def transport_substeps(adjoint, east_a, east_b, north_a, north_b, width):
    fields, levels, columns, lanes = adjoint.shape
    chunk = 5 if levels % 5 == 0 else levels
    field_block = pl.BlockSpec((fields, chunk, columns, lanes), lambda j: (0, j, 0, 0))
    face_block = pl.BlockSpec((chunk, columns, lanes), lambda j: (j, 0, 0))
    return pl.pallas_call(
        substep_kernel,
        grid=(levels // chunk,),
        in_specs=[field_block, face_block, face_block, face_block, face_block],
        out_specs=pl.BlockSpec((fields, chunk, width, lanes), lambda j: (0, j, 0, 0)),
        out_shape=jax.ShapeDtypeStruct((fields, levels, width, lanes), jnp.float32),
    )(adjoint, east_a, east_b, north_a, north_b)


def padded_halo(pieces, width, halo, padded):
    size = lax.axis_size("grid")
    up = [(i, (i + 1) % size) for i in range(size)]
    down = [(j, i) for i, j in up]
    last = jnp.concatenate([piece[:, width - halo :] for piece in pieces], 0)
    initial = jnp.concatenate([piece[:, :halo] for piece in pieces], 0)
    before = lax.ppermute(last, "grid", up)
    after = lax.ppermute(initial, "grid", down)
    wide = []
    offset = 0
    for piece in pieces:
        rows = piece.shape[0]
        fill = jnp.zeros((rows, padded - width - 2 * halo, piece.shape[-1]), jnp.float32)
        wide.append(
            jnp.concatenate(
                [before[offset : offset + rows], piece, after[offset : offset + rows], fill], 1
            )
        )
        offset += rows
    return wide


def on_device(
    adjoint_in,
    surface_carbon,
    surface_alkalinity,
    east_velocity,
    north_velocity,
    east_diffusion,
    north_diffusion,
    vertical_mix,
    thickness,
    export_flux,
    piston,
    wet_mask,
    bottom_level,
):
    levels = vertical_mix.shape[0]
    width = east_velocity.shape[1]
    halo = SUBSTEPS
    padded = -(-(width + 2 * halo) // 8) * 8
    wet_bottom = jnp.where(wet_mask > 0, bottom_level, 0).astype(jnp.float32)
    depth_index = lax.broadcasted_iota(jnp.int32, (levels, padded, wet_bottom.shape[-1]), 0)
    wet_cube = (depth_index[:, :width] < wet_bottom[None]).astype(jnp.float32)

    below_band, diagonal, above_band = column_coefficients(vertical_mix, thickness, wet_cube)
    adjoint = transposed_solve(adjoint_in, below_band, diagonal, above_band)
    adjoint, east_velocity, north_velocity, wet_bottom = lax.optimization_barrier(
        (adjoint, east_velocity, north_velocity, wet_bottom)
    )
    (adjoint,) = padded_halo(
        [adjoint.reshape((-1,) + adjoint.shape[-2:])], width, halo, padded
    )
    wide_east, wide_north, wide_bottom = padded_halo(
        [east_velocity, north_velocity, wet_bottom[None]], width, halo, padded
    )
    wide_wet = (depth_index.astype(jnp.float32) < wide_bottom).astype(jnp.float32)

    east_a, east_b = face_pairs(
        wide_east, wide_wet, jnp.roll(wide_wet, -1, axis=1), east_diffusion
    )
    zero_row = jnp.zeros(wide_wet.shape[:-1] + (1,), jnp.float32)
    north_next = jnp.concatenate([wide_wet[..., 1:], zero_row], -1)
    north_a, north_b = face_pairs(wide_north, wide_wet, north_next, north_diffusion)

    fields = adjoint_in.shape[0] * adjoint_in.shape[1]
    adjoint = transport_substeps(
        adjoint.reshape((fields, levels) + adjoint.shape[-2:]),
        east_a,
        east_b,
        north_a,
        north_b,
        width,
    ).reshape(adjoint_in.shape)
    rate_term = jnp.sum(adjoint[:, 0] - alk_ratio * adjoint[:, 1], axis=0)
    summed = scenario_sum(rate_term)
    rate_gradient = export_flux * wet_cube * summed
    slope_carbon, slope_alkalinity = carbonate_slopes(surface_carbon, surface_alkalinity)
    exchange_scale = wet_cube[0] * piston * adjoint[:, 0, 0]
    adjoint = (
        adjoint.at[:, 0, 0]
        .add(-exchange_scale * slope_carbon)
        .at[:, 1, 0]
        .add(-exchange_scale * slope_alkalinity)
    )
    return (adjoint, rate_gradient)


def solution(mesh):
    in_specs = (
        P("scen", None, None, "grid", None),
        P("scen", "grid", None),
        P("scen", "grid", None),
        P(None, "grid", None),
        P(None, "grid", None),
        P(),
        P(),
        P(None, "grid", None),
        P(),
        P(None, "grid", None),
        P("grid", None),
        P("grid", None),
        P("grid", None),
    )
    out_specs = (P("scen", None, None, "grid", None), P(None, "grid", None))
    return jax.shard_map(
        on_device, mesh=mesh, in_specs=in_specs, out_specs=out_specs, check_vma=False
    )
```

```python
import jax
import jax.numpy as jnp
from jax import lax
from jax.sharding import PartitionSpec as P
from jax.experimental import pallas as pl
from jax.experimental.pallas import tpu as pltpu

SUBSTEPS = 6


alk_ratio = 0.137


def face_pairs(velocity, mask_here, mask_next, diffusion):
    opened = mask_here * mask_next
    moving = velocity * opened
    mixing = diffusion[:, None, None] * opened
    return (mixing + jnp.maximum(moving, 0.0), jnp.minimum(moving, 0.0) - mixing)


def column_coefficients(vertical_mix, thickness, wet_cube):
    zero_layer = jnp.zeros((1,) + wet_cube.shape[1:], jnp.float32)
    opened = jnp.concatenate([wet_cube[:-1] * wet_cube[1:], zero_layer], 0)
    mixing = vertical_mix * opened
    mixing_above = jnp.concatenate([zero_layer, mixing[:-1]], 0)
    height = thickness[:, None, None]
    height_above = jnp.concatenate([thickness[:1], thickness[:-1]])[:, None, None]
    height_below = jnp.concatenate([thickness[1:], thickness[-1:]])[:, None, None]
    diagonal = 1.0 + (mixing + mixing_above) / height
    below_band = -mixing_above / height_above
    above_band = -mixing / height_below
    return (below_band, diagonal, above_band)


def solve_kernel(rhs_ref, below_ref, diagonal_ref, above_ref, out_ref, factor_ref):
    levels = diagonal_ref.shape[0]
    pivots = diagonal_ref[0]
    factor_ref[0] = above_ref[0] / pivots
    reduced = rhs_ref[:, 0] / pivots
    out_ref[:, 0] = reduced
    for level in range(1, levels):
        below = below_ref[level]
        pivots = diagonal_ref[level] - below * factor_ref[level - 1]
        factor_ref[level] = above_ref[level] / pivots
        reduced = (rhs_ref[:, level] - below * reduced) / pivots
        out_ref[:, level] = reduced
    solved = reduced
    for level in range(levels - 2, -1, -1):
        solved = out_ref[:, level] - factor_ref[level] * solved
        out_ref[:, level] = solved


def transposed_solve(right_side, below_band, diagonal, above_band):
    shape = right_side.shape
    rhs = right_side.reshape((-1,) + shape[-3:])
    out = pl.pallas_call(
        solve_kernel,
        out_shape=jax.ShapeDtypeStruct(rhs.shape, jnp.float32),
        scratch_shapes=[pltpu.VMEM(diagonal.shape, jnp.float32)],
    )(rhs, below_band, diagonal, above_band)
    return out.reshape(shape)


def carbonate_slopes(carbon, alkalinity):
    excess = 2.0 * carbon - alkalinity
    spread = alkalinity - carbon
    square = spread * spread
    return (
        (4.0 * excess * spread + excess * excess) / square,
        (-2.0 * excess * spread - excess * excess) / square,
    )


def scenario_sum(field):
    size = lax.axis_size("scen")
    shape = field.shape
    pieces = field.reshape((size, -1, shape[-1]))
    gathered = lax.all_to_all(pieces, "scen", 0, 0, tiled=True)
    owned = jnp.sum(gathered, axis=0)
    spread = jnp.broadcast_to(owned[None], (size,) + owned.shape)
    return lax.all_to_all(spread, "scen", 0, 0, tiled=True).reshape(shape)


def substep_kernel(adjoint_ref, east_a_ref, east_b_ref, north_a_ref, north_b_ref, out_ref):
    columns = adjoint_ref.shape[-2]
    lanes = adjoint_ref.shape[-1]
    east_a = east_a_ref[...]
    east_b_behind = pltpu.roll(east_b_ref[...], 1, 1)
    north_a = north_a_ref[...]
    north_b_behind = pltpu.roll(north_b_ref[...], 1, 2)
    for field in range(adjoint_ref.shape[0]):
        adjoint = adjoint_ref[field]
        for repeat in range(SUBSTEPS):
            ahead = pltpu.roll(adjoint, columns - 1, 1)
            behind = pltpu.roll(adjoint, 1, 1)
            north_ahead = pltpu.roll(adjoint, lanes - 1, 2)
            north_behind = pltpu.roll(adjoint, 1, 2)
            adjoint = (
                adjoint
                - east_a * (adjoint - ahead)
                - east_b_behind * (behind - adjoint)
                - (north_a * (adjoint - north_ahead) + north_b_behind * (north_behind - adjoint))
            )
        aligned = pltpu.roll(adjoint, columns - SUBSTEPS, 1)
        out_ref[field] = aligned[:, : out_ref.shape[-2]]


def transport_substeps(adjoint, east_a, east_b, north_a, north_b, width):
    fields, levels, columns, lanes = adjoint.shape
    chunk = 10 if levels % 10 == 0 else levels
    field_block = pl.BlockSpec((fields, chunk, columns, lanes), lambda j: (0, j, 0, 0))
    face_block = pl.BlockSpec((chunk, columns, lanes), lambda j: (j, 0, 0))
    return pl.pallas_call(
        substep_kernel,
        grid=(levels // chunk,),
        in_specs=[field_block, face_block, face_block, face_block, face_block],
        out_specs=pl.BlockSpec((fields, chunk, width, lanes), lambda j: (0, j, 0, 0)),
        out_shape=jax.ShapeDtypeStruct((fields, levels, width, lanes), jnp.float32),
    )(adjoint, east_a, east_b, north_a, north_b)


def padded_halo(pieces, width, halo, padded):
    size = lax.axis_size("grid")
    up = [(i, (i + 1) % size) for i in range(size)]
    down = [(j, i) for i, j in up]
    last = jnp.concatenate([piece[:, width - halo :] for piece in pieces], 0)
    initial = jnp.concatenate([piece[:, :halo] for piece in pieces], 0)
    before = lax.ppermute(last, "grid", up)
    after = lax.ppermute(initial, "grid", down)
    wide = []
    offset = 0
    for piece in pieces:
        rows = piece.shape[0]
        fill = jnp.zeros((rows, padded - width - 2 * halo, piece.shape[-1]), jnp.float32)
        wide.append(
            jnp.concatenate(
                [before[offset : offset + rows], piece, after[offset : offset + rows], fill], 1
            )
        )
        offset += rows
    return wide


def on_device(
    adjoint_in,
    surface_carbon,
    surface_alkalinity,
    east_velocity,
    north_velocity,
    east_diffusion,
    north_diffusion,
    vertical_mix,
    thickness,
    export_flux,
    piston,
    wet_mask,
    bottom_level,
):
    levels = vertical_mix.shape[0]
    width = east_velocity.shape[1]
    halo = SUBSTEPS
    padded = -(-(width + 2 * halo) // 8) * 8
    wet_bottom = jnp.where(wet_mask > 0, bottom_level, 0).astype(jnp.float32)
    wide_east, wide_north, wide_bottom = padded_halo(
        [east_velocity, north_velocity, wet_bottom[None]], width, halo, padded
    )
    depth_index = lax.broadcasted_iota(jnp.int32, (levels,) + wide_bottom.shape[1:], 0)
    wide_wet = (depth_index.astype(jnp.float32) < wide_bottom).astype(jnp.float32)
    wet_cube = (depth_index[:, :width] < wet_bottom[None]).astype(jnp.float32)

    below_band, diagonal, above_band = column_coefficients(vertical_mix, thickness, wet_cube)
    adjoint = transposed_solve(adjoint_in, below_band, diagonal, above_band)
    (adjoint,) = padded_halo(
        [adjoint.reshape((-1,) + adjoint.shape[-2:])], width, halo, padded
    )

    east_a, east_b = face_pairs(
        wide_east, wide_wet, jnp.roll(wide_wet, -1, axis=1), east_diffusion
    )
    zero_row = jnp.zeros(wide_wet.shape[:-1] + (1,), jnp.float32)
    north_next = jnp.concatenate([wide_wet[..., 1:], zero_row], -1)
    north_a, north_b = face_pairs(wide_north, wide_wet, north_next, north_diffusion)

    fields = adjoint_in.shape[0] * adjoint_in.shape[1]
    adjoint = transport_substeps(
        adjoint.reshape((fields, levels) + adjoint.shape[-2:]),
        east_a,
        east_b,
        north_a,
        north_b,
        width,
    ).reshape(adjoint_in.shape)
    rate_term = jnp.sum(adjoint[:, 0] - alk_ratio * adjoint[:, 1], axis=0)
    summed = scenario_sum(rate_term)
    rate_gradient = export_flux * wet_cube * summed
    slope_carbon, slope_alkalinity = carbonate_slopes(surface_carbon, surface_alkalinity)
    exchange_scale = wet_cube[0] * piston * adjoint[:, 0, 0]
    adjoint = (
        adjoint.at[:, 0, 0]
        .add(-exchange_scale * slope_carbon)
        .at[:, 1, 0]
        .add(-exchange_scale * slope_alkalinity)
    )
    return (adjoint, rate_gradient)


def solution(mesh):
    in_specs = (
        P("scen", None, None, "grid", None),
        P("scen", "grid", None),
        P("scen", "grid", None),
        P(None, "grid", None),
        P(None, "grid", None),
        P(),
        P(),
        P(None, "grid", None),
        P(),
        P(None, "grid", None),
        P("grid", None),
        P("grid", None),
        P("grid", None),
    )
    out_specs = (P("scen", None, None, "grid", None), P(None, "grid", None))
    return jax.shard_map(
        on_device, mesh=mesh, in_specs=in_specs, out_specs=out_specs, check_vma=False
    )
```

```python
import jax
import jax.numpy as jnp
from jax import lax
from jax.sharding import PartitionSpec as P
from jax.experimental import pallas as pl
from jax.experimental.pallas import tpu as pltpu

SUBSTEPS = 6


alk_ratio = 0.137


def face_pairs(velocity, mask_here, mask_next, diffusion):
    opened = mask_here * mask_next
    moving = velocity * opened
    mixing = diffusion[:, None, None] * opened
    return (mixing + jnp.maximum(moving, 0.0), jnp.minimum(moving, 0.0) - mixing)


def column_coefficients(vertical_mix, thickness, wet_cube):
    zero_layer = jnp.zeros((1,) + wet_cube.shape[1:], jnp.float32)
    opened = jnp.concatenate([wet_cube[:-1] * wet_cube[1:], zero_layer], 0)
    mixing = vertical_mix * opened
    mixing_above = jnp.concatenate([zero_layer, mixing[:-1]], 0)
    height = thickness[:, None, None]
    height_above = jnp.concatenate([thickness[:1], thickness[:-1]])[:, None, None]
    height_below = jnp.concatenate([thickness[1:], thickness[-1:]])[:, None, None]
    diagonal = 1.0 + (mixing + mixing_above) / height
    below_band = -mixing_above / height_above
    above_band = -mixing / height_below
    return (below_band, diagonal, above_band)


def solve_kernel(rhs_ref, below_ref, diagonal_ref, above_ref, out_ref, factor_ref):
    levels = diagonal_ref.shape[0]
    pivots = diagonal_ref[0]
    factor_ref[0] = above_ref[0] / pivots
    reduced = rhs_ref[:, 0] / pivots
    out_ref[:, 0] = reduced
    for level in range(1, levels):
        below = below_ref[level]
        pivots = diagonal_ref[level] - below * factor_ref[level - 1]
        factor_ref[level] = above_ref[level] / pivots
        reduced = (rhs_ref[:, level] - below * reduced) / pivots
        out_ref[:, level] = reduced
    solved = reduced
    for level in range(levels - 2, -1, -1):
        solved = out_ref[:, level] - factor_ref[level] * solved
        out_ref[:, level] = solved


def transposed_solve(right_side, below_band, diagonal, above_band):
    shape = right_side.shape
    rhs = right_side.reshape((-1,) + shape[-3:])
    out = pl.pallas_call(
        solve_kernel,
        out_shape=jax.ShapeDtypeStruct(rhs.shape, jnp.float32),
        scratch_shapes=[pltpu.VMEM(diagonal.shape, jnp.float32)],
    )(rhs, below_band, diagonal, above_band)
    return out.reshape(shape)


def carbonate_slopes(carbon, alkalinity):
    excess = 2.0 * carbon - alkalinity
    spread = alkalinity - carbon
    square = spread * spread
    return (
        (4.0 * excess * spread + excess * excess) / square,
        (-2.0 * excess * spread - excess * excess) / square,
    )


def scenario_sum(field):
    size = lax.axis_size("scen")
    shape = field.shape
    pieces = field.reshape((size, -1, shape[-1]))
    gathered = lax.all_to_all(pieces, "scen", 0, 0, tiled=True)
    owned = jnp.sum(gathered, axis=0)
    spread = jnp.broadcast_to(owned[None], (size,) + owned.shape)
    return lax.all_to_all(spread, "scen", 0, 0, tiled=True).reshape(shape)


def substep_kernel(adjoint_ref, east_a_ref, east_b_ref, north_a_ref, north_b_ref, out_ref):
    columns = adjoint_ref.shape[-2]
    lanes = adjoint_ref.shape[-1]
    east_a = east_a_ref[...]
    east_b_behind = pltpu.roll(east_b_ref[...], 1, 1)
    north_a = north_a_ref[...]
    north_b_behind = pltpu.roll(north_b_ref[...], 1, 2)
    for field in range(adjoint_ref.shape[0]):
        adjoint = adjoint_ref[field]
        for repeat in range(SUBSTEPS):
            ahead = pltpu.roll(adjoint, columns - 1, 1)
            behind = pltpu.roll(adjoint, 1, 1)
            north_ahead = pltpu.roll(adjoint, lanes - 1, 2)
            north_behind = pltpu.roll(adjoint, 1, 2)
            adjoint = (
                adjoint
                - east_a * (adjoint - ahead)
                - east_b_behind * (behind - adjoint)
                - (north_a * (adjoint - north_ahead) + north_b_behind * (north_behind - adjoint))
            )
        aligned = pltpu.roll(adjoint, columns - SUBSTEPS, 1)
        out_ref[field] = aligned[:, : out_ref.shape[-2]]


def transport_substeps(adjoint, east_a, east_b, north_a, north_b, width):
    fields, levels, columns, lanes = adjoint.shape
    chunk = 25 if levels % 25 == 0 else levels
    field_block = pl.BlockSpec((fields, chunk, columns, lanes), lambda j: (0, j, 0, 0))
    face_block = pl.BlockSpec((chunk, columns, lanes), lambda j: (j, 0, 0))
    return pl.pallas_call(
        substep_kernel,
        grid=(levels // chunk,),
        in_specs=[field_block, face_block, face_block, face_block, face_block],
        out_specs=pl.BlockSpec((fields, chunk, width, lanes), lambda j: (0, j, 0, 0)),
        out_shape=jax.ShapeDtypeStruct((fields, levels, width, lanes), jnp.float32),
    )(adjoint, east_a, east_b, north_a, north_b)


def padded_halo(pieces, width, halo, padded):
    size = lax.axis_size("grid")
    up = [(i, (i + 1) % size) for i in range(size)]
    down = [(j, i) for i, j in up]
    last = jnp.concatenate([piece[:, width - halo :] for piece in pieces], 0)
    initial = jnp.concatenate([piece[:, :halo] for piece in pieces], 0)
    before = lax.ppermute(last, "grid", up)
    after = lax.ppermute(initial, "grid", down)
    wide = []
    offset = 0
    for piece in pieces:
        rows = piece.shape[0]
        fill = jnp.zeros((rows, padded - width - 2 * halo, piece.shape[-1]), jnp.float32)
        wide.append(
            jnp.concatenate(
                [before[offset : offset + rows], piece, after[offset : offset + rows], fill], 1
            )
        )
        offset += rows
    return wide


def on_device(
    adjoint_in,
    surface_carbon,
    surface_alkalinity,
    east_velocity,
    north_velocity,
    east_diffusion,
    north_diffusion,
    vertical_mix,
    thickness,
    export_flux,
    piston,
    wet_mask,
    bottom_level,
):
    levels = vertical_mix.shape[0]
    width = east_velocity.shape[1]
    halo = SUBSTEPS
    padded = -(-(width + 2 * halo) // 8) * 8
    wet_bottom = jnp.where(wet_mask > 0, bottom_level, 0).astype(jnp.float32)
    wide_east, wide_north, wide_bottom = padded_halo(
        [east_velocity, north_velocity, wet_bottom[None]], width, halo, padded
    )
    depth_index = lax.broadcasted_iota(jnp.int32, (levels,) + wide_bottom.shape[1:], 0)
    wide_wet = (depth_index.astype(jnp.float32) < wide_bottom).astype(jnp.float32)
    wet_cube = (depth_index[:, :width] < wet_bottom[None]).astype(jnp.float32)

    below_band, diagonal, above_band = column_coefficients(vertical_mix, thickness, wet_cube)
    adjoint = transposed_solve(adjoint_in, below_band, diagonal, above_band)
    (adjoint,) = padded_halo(
        [adjoint.reshape((-1,) + adjoint.shape[-2:])], width, halo, padded
    )

    east_a, east_b = face_pairs(
        wide_east, wide_wet, jnp.roll(wide_wet, -1, axis=1), east_diffusion
    )
    zero_row = jnp.zeros(wide_wet.shape[:-1] + (1,), jnp.float32)
    north_next = jnp.concatenate([wide_wet[..., 1:], zero_row], -1)
    north_a, north_b = face_pairs(wide_north, wide_wet, north_next, north_diffusion)

    fields = adjoint_in.shape[0] * adjoint_in.shape[1]
    adjoint = transport_substeps(
        adjoint.reshape((fields, levels) + adjoint.shape[-2:]),
        east_a,
        east_b,
        north_a,
        north_b,
        width,
    ).reshape(adjoint_in.shape)
    rate_term = jnp.sum(adjoint[:, 0] - alk_ratio * adjoint[:, 1], axis=0)
    summed = scenario_sum(rate_term)
    rate_gradient = export_flux * wet_cube * summed
    slope_carbon, slope_alkalinity = carbonate_slopes(surface_carbon, surface_alkalinity)
    exchange_scale = wet_cube[0] * piston * adjoint[:, 0, 0]
    adjoint = (
        adjoint.at[:, 0, 0]
        .add(-exchange_scale * slope_carbon)
        .at[:, 1, 0]
        .add(-exchange_scale * slope_alkalinity)
    )
    return (adjoint, rate_gradient)


def solution(mesh):
    in_specs = (
        P("scen", None, None, "grid", None),
        P("scen", "grid", None),
        P("scen", "grid", None),
        P(None, "grid", None),
        P(None, "grid", None),
        P(),
        P(),
        P(None, "grid", None),
        P(),
        P(None, "grid", None),
        P("grid", None),
        P("grid", None),
        P("grid", None),
    )
    out_specs = (P("scen", None, None, "grid", None), P(None, "grid", None))
    return jax.shard_map(
        on_device, mesh=mesh, in_specs=in_specs, out_specs=out_specs, check_vma=False
    )
```

```python
import jax
import jax.numpy as jnp
from jax import lax
from jax.sharding import PartitionSpec as P
from jax.experimental import pallas as pl
from jax.experimental.pallas import tpu as pltpu

SUBSTEPS = 6


alk_ratio = 0.137


def face_pairs(velocity, mask_here, mask_next, diffusion):
    opened = mask_here * mask_next
    moving = velocity * opened
    mixing = diffusion[:, None, None] * opened
    return (mixing + jnp.maximum(moving, 0.0), jnp.minimum(moving, 0.0) - mixing)


def column_coefficients(vertical_mix, thickness, wet_cube):
    zero_layer = jnp.zeros((1,) + wet_cube.shape[1:], jnp.float32)
    opened = jnp.concatenate([wet_cube[:-1] * wet_cube[1:], zero_layer], 0)
    mixing = vertical_mix * opened
    mixing_above = jnp.concatenate([zero_layer, mixing[:-1]], 0)
    height = thickness[:, None, None]
    height_above = jnp.concatenate([thickness[:1], thickness[:-1]])[:, None, None]
    height_below = jnp.concatenate([thickness[1:], thickness[-1:]])[:, None, None]
    diagonal = 1.0 + (mixing + mixing_above) / height
    below_band = -mixing_above / height_above
    above_band = -mixing / height_below
    return (below_band, diagonal, above_band)


def solve_kernel(rhs_ref, below_ref, diagonal_ref, above_ref, out_ref, factor_ref):
    levels = diagonal_ref.shape[0]
    pivots = diagonal_ref[0]
    factor_ref[0] = above_ref[0] / pivots
    reduced = rhs_ref[:, 0] / pivots
    out_ref[:, 0] = reduced
    for level in range(1, levels):
        below = below_ref[level]
        pivots = diagonal_ref[level] - below * factor_ref[level - 1]
        factor_ref[level] = above_ref[level] / pivots
        reduced = (rhs_ref[:, level] - below * reduced) / pivots
        out_ref[:, level] = reduced
    solved = reduced
    for level in range(levels - 2, -1, -1):
        solved = out_ref[:, level] - factor_ref[level] * solved
        out_ref[:, level] = solved


def transposed_solve(right_side, below_band, diagonal, above_band):
    shape = right_side.shape
    rhs = right_side.reshape((-1,) + shape[-3:])
    out = pl.pallas_call(
        solve_kernel,
        out_shape=jax.ShapeDtypeStruct(rhs.shape, jnp.float32),
        scratch_shapes=[pltpu.VMEM(diagonal.shape, jnp.float32)],
    )(rhs, below_band, diagonal, above_band)
    return out.reshape(shape)


def carbonate_slopes(carbon, alkalinity):
    excess = 2.0 * carbon - alkalinity
    spread = alkalinity - carbon
    square = spread * spread
    return (
        (4.0 * excess * spread + excess * excess) / square,
        (-2.0 * excess * spread - excess * excess) / square,
    )


def scenario_sum(field):
    size = lax.axis_size("scen")
    shape = field.shape
    pieces = field.reshape((size, -1, shape[-1]))
    gathered = lax.all_to_all(pieces, "scen", 0, 0, tiled=True)
    owned = jnp.sum(gathered, axis=0)
    spread = jnp.broadcast_to(owned[None], (size,) + owned.shape)
    return lax.all_to_all(spread, "scen", 0, 0, tiled=True).reshape(shape)


def substep_kernel(adjoint_ref, east_a_ref, east_b_ref, north_a_ref, north_b_ref, out_ref):
    columns = adjoint_ref.shape[-2]
    lanes = adjoint_ref.shape[-1]
    east_a = east_a_ref[...]
    east_b_behind = pltpu.roll(east_b_ref[...], 1, 1)
    north_a = north_a_ref[...]
    north_b_behind = pltpu.roll(north_b_ref[...], 1, 2)
    for field in range(adjoint_ref.shape[0]):
        adjoint = adjoint_ref[field]
        for repeat in range(SUBSTEPS):
            ahead = pltpu.roll(adjoint, columns - 1, 1)
            behind = pltpu.roll(adjoint, 1, 1)
            north_ahead = pltpu.roll(adjoint, lanes - 1, 2)
            north_behind = pltpu.roll(adjoint, 1, 2)
            adjoint = (
                adjoint
                - east_a * (adjoint - ahead)
                - east_b_behind * (behind - adjoint)
                - (north_a * (adjoint - north_ahead) + north_b_behind * (north_behind - adjoint))
            )
        aligned = pltpu.roll(adjoint, columns - SUBSTEPS, 1)
        out_ref[field] = aligned[:, : out_ref.shape[-2]]


def transport_substeps(adjoint, east_a, east_b, north_a, north_b, width):
    fields, levels, columns, lanes = adjoint.shape
    chunk = levels
    field_block = pl.BlockSpec((fields, chunk, columns, lanes), lambda j: (0, j, 0, 0))
    face_block = pl.BlockSpec((chunk, columns, lanes), lambda j: (j, 0, 0))
    return pl.pallas_call(
        substep_kernel,
        grid=(levels // chunk,),
        in_specs=[field_block, face_block, face_block, face_block, face_block],
        out_specs=pl.BlockSpec((fields, chunk, width, lanes), lambda j: (0, j, 0, 0)),
        out_shape=jax.ShapeDtypeStruct((fields, levels, width, lanes), jnp.float32),
    )(adjoint, east_a, east_b, north_a, north_b)


def padded_halo(pieces, width, halo, padded):
    size = lax.axis_size("grid")
    up = [(i, (i + 1) % size) for i in range(size)]
    down = [(j, i) for i, j in up]
    last = jnp.concatenate([piece[:, width - halo :] for piece in pieces], 0)
    initial = jnp.concatenate([piece[:, :halo] for piece in pieces], 0)
    before = lax.ppermute(last, "grid", up)
    after = lax.ppermute(initial, "grid", down)
    wide = []
    offset = 0
    for piece in pieces:
        rows = piece.shape[0]
        fill = jnp.zeros((rows, padded - width - 2 * halo, piece.shape[-1]), jnp.float32)
        wide.append(
            jnp.concatenate(
                [before[offset : offset + rows], piece, after[offset : offset + rows], fill], 1
            )
        )
        offset += rows
    return wide


def on_device(
    adjoint_in,
    surface_carbon,
    surface_alkalinity,
    east_velocity,
    north_velocity,
    east_diffusion,
    north_diffusion,
    vertical_mix,
    thickness,
    export_flux,
    piston,
    wet_mask,
    bottom_level,
):
    levels = vertical_mix.shape[0]
    width = east_velocity.shape[1]
    halo = SUBSTEPS
    padded = -(-(width + 2 * halo) // 8) * 8
    wet_bottom = jnp.where(wet_mask > 0, bottom_level, 0).astype(jnp.float32)
    wide_east, wide_north, wide_bottom = padded_halo(
        [east_velocity, north_velocity, wet_bottom[None]], width, halo, padded
    )
    depth_index = lax.broadcasted_iota(jnp.int32, (levels,) + wide_bottom.shape[1:], 0)
    wide_wet = (depth_index.astype(jnp.float32) < wide_bottom).astype(jnp.float32)
    wet_cube = (depth_index[:, :width] < wet_bottom[None]).astype(jnp.float32)

    below_band, diagonal, above_band = column_coefficients(vertical_mix, thickness, wet_cube)
    adjoint = transposed_solve(adjoint_in, below_band, diagonal, above_band)
    (adjoint,) = padded_halo(
        [adjoint.reshape((-1,) + adjoint.shape[-2:])], width, halo, padded
    )

    east_a, east_b = face_pairs(
        wide_east, wide_wet, jnp.roll(wide_wet, -1, axis=1), east_diffusion
    )
    zero_row = jnp.zeros(wide_wet.shape[:-1] + (1,), jnp.float32)
    north_next = jnp.concatenate([wide_wet[..., 1:], zero_row], -1)
    north_a, north_b = face_pairs(wide_north, wide_wet, north_next, north_diffusion)

    fields = adjoint_in.shape[0] * adjoint_in.shape[1]
    adjoint = transport_substeps(
        adjoint.reshape((fields, levels) + adjoint.shape[-2:]),
        east_a,
        east_b,
        north_a,
        north_b,
        width,
    ).reshape(adjoint_in.shape)
    rate_term = jnp.sum(adjoint[:, 0] - alk_ratio * adjoint[:, 1], axis=0)
    summed = scenario_sum(rate_term)
    rate_gradient = export_flux * wet_cube * summed
    slope_carbon, slope_alkalinity = carbonate_slopes(surface_carbon, surface_alkalinity)
    exchange_scale = wet_cube[0] * piston * adjoint[:, 0, 0]
    adjoint = (
        adjoint.at[:, 0, 0]
        .add(-exchange_scale * slope_carbon)
        .at[:, 1, 0]
        .add(-exchange_scale * slope_alkalinity)
    )
    return (adjoint, rate_gradient)


def solution(mesh):
    in_specs = (
        P("scen", None, None, "grid", None),
        P("scen", "grid", None),
        P("scen", "grid", None),
        P(None, "grid", None),
        P(None, "grid", None),
        P(),
        P(),
        P(None, "grid", None),
        P(),
        P(None, "grid", None),
        P("grid", None),
        P("grid", None),
        P("grid", None),
    )
    out_specs = (P("scen", None, None, "grid", None), P(None, "grid", None))
    return jax.shard_map(
        on_device, mesh=mesh, in_specs=in_specs, out_specs=out_specs, check_vma=False
    )
```

```python
import jax
import jax.numpy as jnp
from jax import lax
from jax.sharding import PartitionSpec as P
from jax.experimental import pallas as pl
from jax.experimental.pallas import tpu as pltpu

SUBSTEPS = 6


alk_ratio = 0.137


def face_pairs(velocity, mask_here, mask_next, diffusion):
    opened = mask_here * mask_next
    moving = velocity * opened
    mixing = diffusion[:, None, None] * opened
    return (mixing + jnp.maximum(moving, 0.0), jnp.minimum(moving, 0.0) - mixing)


def column_coefficients(vertical_mix, thickness, wet_cube):
    zero_layer = jnp.zeros((1,) + wet_cube.shape[1:], jnp.float32)
    opened = jnp.concatenate([wet_cube[:-1] * wet_cube[1:], zero_layer], 0)
    mixing = vertical_mix * opened
    mixing_above = jnp.concatenate([zero_layer, mixing[:-1]], 0)
    height = thickness[:, None, None]
    height_above = jnp.concatenate([thickness[:1], thickness[:-1]])[:, None, None]
    height_below = jnp.concatenate([thickness[1:], thickness[-1:]])[:, None, None]
    diagonal = 1.0 + (mixing + mixing_above) / height
    below_band = -mixing_above / height_above
    above_band = -mixing / height_below
    return (below_band, diagonal, above_band)


def solve_kernel(rhs_ref, below_ref, diagonal_ref, above_ref, out_ref, factor_ref):
    levels = diagonal_ref.shape[0]
    pivots = diagonal_ref[0]
    factor_ref[0] = above_ref[0] / pivots
    reduced = rhs_ref[:, 0] / pivots
    out_ref[:, 0] = reduced
    for level in range(1, levels):
        below = below_ref[level]
        pivots = diagonal_ref[level] - below * factor_ref[level - 1]
        factor_ref[level] = above_ref[level] / pivots
        reduced = (rhs_ref[:, level] - below * reduced) / pivots
        out_ref[:, level] = reduced
    solved = reduced
    for level in range(levels - 2, -1, -1):
        solved = out_ref[:, level] - factor_ref[level] * solved
        out_ref[:, level] = solved


def transposed_solve(right_side, below_band, diagonal, above_band):
    shape = right_side.shape
    rhs = right_side.reshape((-1,) + shape[-3:])
    out = pl.pallas_call(
        solve_kernel,
        out_shape=jax.ShapeDtypeStruct(rhs.shape, jnp.float32),
        scratch_shapes=[pltpu.VMEM(diagonal.shape, jnp.float32)],
    )(rhs, below_band, diagonal, above_band)
    return out.reshape(shape)


def carbonate_slopes(carbon, alkalinity):
    excess = 2.0 * carbon - alkalinity
    spread = alkalinity - carbon
    square = spread * spread
    return (
        (4.0 * excess * spread + excess * excess) / square,
        (-2.0 * excess * spread - excess * excess) / square,
    )


def scenario_sum(field):
    size = lax.axis_size("scen")
    shape = field.shape
    pieces = field.reshape((size, -1, shape[-1]))
    gathered = lax.all_to_all(pieces, "scen", 0, 0, tiled=True)
    owned = jnp.sum(gathered, axis=0)
    spread = jnp.broadcast_to(owned[None], (size,) + owned.shape)
    return lax.all_to_all(spread, "scen", 0, 0, tiled=True).reshape(shape)


def substep_kernel(adjoint_ref, east_a_ref, east_b_ref, north_a_ref, north_b_ref, out_ref):
    columns = adjoint_ref.shape[-2]
    lanes = adjoint_ref.shape[-1]
    east_a = east_a_ref[...]
    east_b_behind = pltpu.roll(east_b_ref[...], 1, 1)
    north_a = north_a_ref[...]
    north_b_behind = pltpu.roll(north_b_ref[...], 1, 2)
    for field in range(adjoint_ref.shape[0]):
        adjoint = adjoint_ref[field]
        for repeat in range(SUBSTEPS):
            ahead = pltpu.roll(adjoint, columns - 1, 1)
            behind = pltpu.roll(adjoint, 1, 1)
            north_ahead = pltpu.roll(adjoint, lanes - 1, 2)
            north_behind = pltpu.roll(adjoint, 1, 2)
            adjoint = (
                adjoint
                - east_a * (adjoint - ahead)
                - east_b_behind * (behind - adjoint)
                - (north_a * (adjoint - north_ahead) + north_b_behind * (north_behind - adjoint))
            )
        aligned = pltpu.roll(adjoint, columns - SUBSTEPS, 1)
        out_ref[field] = aligned[:, : out_ref.shape[-2]]


def transport_substeps(adjoint, east_a, east_b, north_a, north_b, width):
    fields, levels, columns, lanes = adjoint.shape
    field_block = pl.BlockSpec((1, levels, columns, lanes), lambda j: (j, 0, 0, 0))
    face_block = pl.BlockSpec((levels, columns, lanes), lambda j: (0, 0, 0))
    return pl.pallas_call(
        substep_kernel,
        grid=(fields,),
        in_specs=[field_block, face_block, face_block, face_block, face_block],
        out_specs=pl.BlockSpec((1, levels, width, lanes), lambda j: (j, 0, 0, 0)),
        out_shape=jax.ShapeDtypeStruct((fields, levels, width, lanes), jnp.float32),
    )(adjoint, east_a, east_b, north_a, north_b)


def padded_halo(pieces, width, halo, padded):
    size = lax.axis_size("grid")
    up = [(i, (i + 1) % size) for i in range(size)]
    down = [(j, i) for i, j in up]
    last = jnp.concatenate([piece[:, width - halo :] for piece in pieces], 0)
    initial = jnp.concatenate([piece[:, :halo] for piece in pieces], 0)
    before = lax.ppermute(last, "grid", up)
    after = lax.ppermute(initial, "grid", down)
    wide = []
    offset = 0
    for piece in pieces:
        rows = piece.shape[0]
        fill = jnp.zeros((rows, padded - width - 2 * halo, piece.shape[-1]), jnp.float32)
        wide.append(
            jnp.concatenate(
                [before[offset : offset + rows], piece, after[offset : offset + rows], fill], 1
            )
        )
        offset += rows
    return wide


def on_device(
    adjoint_in,
    surface_carbon,
    surface_alkalinity,
    east_velocity,
    north_velocity,
    east_diffusion,
    north_diffusion,
    vertical_mix,
    thickness,
    export_flux,
    piston,
    wet_mask,
    bottom_level,
):
    levels = vertical_mix.shape[0]
    width = east_velocity.shape[1]
    halo = SUBSTEPS
    padded = -(-(width + 2 * halo) // 8) * 8
    wet_bottom = jnp.where(wet_mask > 0, bottom_level, 0).astype(jnp.float32)
    wide_east, wide_north, wide_bottom = padded_halo(
        [east_velocity, north_velocity, wet_bottom[None]], width, halo, padded
    )
    depth_index = lax.broadcasted_iota(jnp.int32, (levels,) + wide_bottom.shape[1:], 0)
    wide_wet = (depth_index.astype(jnp.float32) < wide_bottom).astype(jnp.float32)
    wet_cube = (depth_index[:, :width] < wet_bottom[None]).astype(jnp.float32)

    below_band, diagonal, above_band = column_coefficients(vertical_mix, thickness, wet_cube)
    adjoint = transposed_solve(adjoint_in, below_band, diagonal, above_band)
    (adjoint,) = padded_halo(
        [adjoint.reshape((-1,) + adjoint.shape[-2:])], width, halo, padded
    )

    east_a, east_b = face_pairs(
        wide_east, wide_wet, jnp.roll(wide_wet, -1, axis=1), east_diffusion
    )
    zero_row = jnp.zeros(wide_wet.shape[:-1] + (1,), jnp.float32)
    north_next = jnp.concatenate([wide_wet[..., 1:], zero_row], -1)
    north_a, north_b = face_pairs(wide_north, wide_wet, north_next, north_diffusion)

    fields = adjoint_in.shape[0] * adjoint_in.shape[1]
    adjoint = transport_substeps(
        adjoint.reshape((fields, levels) + adjoint.shape[-2:]),
        east_a,
        east_b,
        north_a,
        north_b,
        width,
    ).reshape(adjoint_in.shape)
    rate_term = jnp.sum(adjoint[:, 0] - alk_ratio * adjoint[:, 1], axis=0)
    summed = scenario_sum(rate_term)
    rate_gradient = export_flux * wet_cube * summed
    slope_carbon, slope_alkalinity = carbonate_slopes(surface_carbon, surface_alkalinity)
    exchange_scale = wet_cube[0] * piston * adjoint[:, 0, 0]
    adjoint = (
        adjoint.at[:, 0, 0]
        .add(-exchange_scale * slope_carbon)
        .at[:, 1, 0]
        .add(-exchange_scale * slope_alkalinity)
    )
    return (adjoint, rate_gradient)


def solution(mesh):
    in_specs = (
        P("scen", None, None, "grid", None),
        P("scen", "grid", None),
        P("scen", "grid", None),
        P(None, "grid", None),
        P(None, "grid", None),
        P(),
        P(),
        P(None, "grid", None),
        P(),
        P(None, "grid", None),
        P("grid", None),
        P("grid", None),
        P("grid", None),
    )
    out_specs = (P("scen", None, None, "grid", None), P(None, "grid", None))
    return jax.shard_map(
        on_device, mesh=mesh, in_specs=in_specs, out_specs=out_specs, check_vma=False
    )
```
